256 devices in a mesh: dp: 32 (over x, z_hi, core), tensor: 8 (over y, z_lo).
Axes of the slice: x: 4, y: 4, z: 8 (z_hi: 4, z_lo: 2; z = z_hi * 2 + z_lo), core: 2. Of those that a mesh axis runs over, the one named last changes fastest.
Arguments:
- stream: bfloat16 [64, 430, 2048], P('dp', None, 'tensor'), may hold values from -3 to 3
- normed: bfloat16 [64, 430, 2048], P('dp'), may hold values from -6 to 6
- query_weight: bfloat16 [2048, 2048], P(None, 'tensor'), as said below
- key_weight: bfloat16 [2048, 2048], P(None, 'tensor'), as said below
- value_weight: bfloat16 [2048, 2048], P(None, 'tensor'), may hold values from -0.125 to 0.125
- out_weight: bfloat16 [2048, 2048], P('tensor'), may hold values from -0.125 to 0.125
- norm_gain: bfloat16 [2048], P('tensor'), may hold values from 0.099609375 to 1.8984375
- proj_weight: bfloat16 [2048, 1024], P('tensor'), may hold values from -0.125 to 0.125
- images: bfloat16 [64, 1024], P('dp'), may hold values from -6 to 6
Outputs:
- mean_loss: float32 [], replicated
- grad_normed: bfloat16 [64, 430, 2048], P('dp', None, 'tensor')
- grad_query: float32 [2048, 2048], P('dp', 'tensor')
- grad_key: float32 [2048, 2048], P('dp', 'tensor')
- grad_value: float32 [2048, 2048], P('dp', 'tensor')
- grad_out: float32 [2048, 2048], P('tensor', 'dp')
- grad_proj: float32 [2048, 1024], P('tensor', 'dp')
The draws below stay inside these ranges and needn't reach their ends.
Inputs may be any that keep to these rules, and one draw needn't show every extreme that they name: `query_weight`: query projection entries, independent draws of order 2048^-0.5. `key_weight`: key projection entries, of order 2048^-0.5, in some heads up to about sixteen times that, possibly aligned with the query projection.
All inputs are finite; a program needn't handle non-finite values.
Results may differ from the reference program's by a relative error of at most 0.02.
Values may be sent and summed in bfloat16 or wider, within the bound.
No kernel may reach another device: no remote copies, remote signals or barrier semaphores. Data moves between devices by JAX's collectives and lax.ppermute only.
A program may use at most 128 MiB of HBM per device.

```python
import jax
import jax.numpy as jnp
from jax import lax

D = 2048
H = 16
E = 1024
L = 430
B = 64
N_TENSOR = 8


def weight_pair(key):
    base = jax.random.fold_in(key, 71)
    spread = 1.5 * D ** (-0.5)
    first = jnp.clip(jax.random.normal(jax.random.fold_in(base, 1), (D, D), jnp.float32), -4.0, 4.0) * spread
    noise = jnp.clip(jax.random.normal(jax.random.fold_in(base, 2), (D, D), jnp.float32), -4.0, 4.0) * spread
    second = noise
    return (first, second)


def draw_query_weight(key, part):
    return weight_pair(key)[0].astype(jnp.bfloat16)


def draw_key_weight(key, part):
    return weight_pair(key)[1].astype(jnp.bfloat16)


def strengthened(entries, stream_key, source, target, shards_of, factor):
    owner, partner = [(jnp.arange(entries.shape[dim]) // (entries.shape[dim] // shards_of)).reshape([-1 if axis == dim else 1 for axis in range(entries.ndim)]) for dim in (source, target)]
    chosen = jax.random.permutation(stream_key, shards_of)[partner]
    strong = (owner == chosen) | (owner == (partner + shards_of // 2) % shards_of)
    return jnp.where(strong, factor * entries, entries)


def block_scale(stream_key, dims, cuts, smallest, largest):
    def one(position, shards_of):
        heights = jax.random.uniform(jax.random.fold_in(jax.random.fold_in(stream_key, 6), position), (shards_of,), jnp.float32, smallest / len(cuts), largest / len(cuts))
        return jnp.repeat(jnp.exp(heights), dims[position] // shards_of).reshape((-1,) + (1,) * (len(dims) - position - 1))

    factor_of = one(*cuts[0])
    for cut in cuts[1:]:
        factor_of = factor_of * one(*cut)
    return factor_of


def centred(own_key, dims, scale, bound, split=(), held_as=jnp.bfloat16):
    factor_of = block_scale(own_key, dims, split, -0.22, 0.18) if split else 1.0
    drawn = jax.random.normal(own_key, dims, jnp.float32) * scale * factor_of
    return jnp.minimum(jnp.maximum(drawn, -bound), bound).astype(held_as)


def bell_draw_with(stream_key, dims, scale, limit, pieces, heavy, held_as=jnp.bfloat16):
    array = scale * jax.random.normal(stream_key, dims, jnp.float32)
    if pieces:
        array = array * block_scale(stream_key, dims, pieces, -0.22, 0.18)
    return jnp.clip(strengthened(array, jax.random.fold_in(stream_key, 3), *heavy), -limit, limit).astype(held_as)


def setup_inputs(seed: int = 0) -> dict:
    splits = jax.random.split(jax.random.key(seed), 10)
    stream = centred(splits[0], (B, L, D), 0.5, 3.0, ((0, 32), (2, 8)))
    normed = bell_draw_with(splits[1], (B, L, D), 1.0, 6.0, ((0, 32),), (0, 2, 32, 2.75))
    query_weight = draw_query_weight(jax.random.fold_in(splits[9], 71), 0)
    key_weight = draw_key_weight(jax.random.fold_in(splits[9], 71), 0)
    value_weight = centred(splits[4], (D, D), D ** -0.5, 0.125, ((1, 8),))
    out_weight = centred(splits[5], (D, D), D ** -0.5, 0.125, ((0, 8),))
    norm_gain = jnp.clip(1.0 + 0.18 * jax.random.normal(splits[6], (D,), jnp.float32), 0.099609375, 1.8984375).astype(jnp.bfloat16)
    proj_weight = centred(splits[7], (D, E), D ** -0.5, 0.125, ((0, 8),))
    images = centred(splits[8], (B, E), 1.0, 6.0, ((0, 32),))
    return {"stream": stream, "normed": normed, "query_weight": query_weight, "key_weight": key_weight, "value_weight": value_weight, "out_weight": out_weight, "norm_gain": norm_gain, "proj_weight": proj_weight, "images": images}


SCALE_LOGIT = 14.0
GRAD_SCALE = 256.0
EPSILON = 1e-05
HIGH = lax.Precision.HIGHEST

def attend(sequence, query_weight, key_weight, value_weight):
    head_size = D // H
    queries = jnp.dot(sequence, query_weight, preferred_element_type=jnp.float32).astype(jnp.bfloat16)
    keys_all = jnp.dot(sequence, key_weight, preferred_element_type=jnp.float32).astype(jnp.bfloat16)
    values_all = jnp.dot(sequence, value_weight, preferred_element_type=jnp.float32).astype(jnp.bfloat16)
    queries = queries.reshape(L, H, head_size)
    keys_all = keys_all.reshape(L, H, head_size)
    values_all = values_all.reshape(L, H, head_size)
    scores = jnp.einsum('qhd,khd->hqk', queries.astype(jnp.float32), keys_all.astype(jnp.float32)) * head_size ** (-0.5)
    row_max = lax.optimization_barrier(jnp.max(scores, axis=-1, keepdims=True))
    exp_scores = jnp.exp(scores - row_max)
    attn_prob = exp_scores / lax.optimization_barrier(jnp.sum(exp_scores, axis=-1, keepdims=True))
    attn_half = attn_prob.astype(jnp.bfloat16)
    return (queries, keys_all, values_all, attn_prob, attn_half)

def reference(stream, normed, query_weight, key_weight, value_weight, out_weight, norm_gain, proj_weight, images):
    head_size = D // H
    group_cols = D // N_TENSOR

    def forward_one(sequence):
        queries, keys_all, values_all, attn_prob, attn_half = attend(sequence, query_weight, key_weight, value_weight)
        heads_out = jnp.einsum('hqk,khd->qhd', attn_half.astype(jnp.float32), values_all.astype(jnp.float32))
        return heads_out.astype(jnp.bfloat16).reshape(L, D)
    head_concat = lax.map(forward_one, normed)
    attended = lax.map(lambda rows: jnp.dot(rows, out_weight, preferred_element_type=jnp.float32), head_concat)
    residual = stream.astype(jnp.float32) + attended
    center = lax.optimization_barrier(jnp.mean(residual, axis=-1, keepdims=True))
    offset = residual - center
    variance = lax.optimization_barrier(jnp.mean(offset * offset, axis=-1, keepdims=True))
    inv_std = lax.rsqrt(variance + EPSILON)
    normal_feat = offset * inv_std
    gain_float = norm_gain.astype(jnp.float32)
    pooled = lax.optimization_barrier(jnp.mean(normal_feat * gain_float, axis=1)).astype(jnp.bfloat16)
    embedded = jnp.dot(pooled, proj_weight, preferred_element_type=jnp.float32)
    embed_norm = jnp.sqrt(lax.optimization_barrier(jnp.sum(embedded * embedded, axis=-1, keepdims=True)) + EPSILON)
    spectra = embedded / embed_norm
    image_float = images.astype(jnp.float32)
    image_unit = image_float / jnp.sqrt(lax.optimization_barrier(jnp.sum(image_float * image_float, axis=-1, keepdims=True)) + EPSILON)
    logits = SCALE_LOGIT * jnp.dot(spectra, image_unit.T, precision=HIGH)
    row_lse = jnp.log(lax.optimization_barrier(jnp.sum(jnp.exp(logits), axis=1)))
    col_lse = jnp.log(lax.optimization_barrier(jnp.sum(jnp.exp(logits), axis=0)))
    count = logits.shape[0]
    mean_loss = (0.5 * jnp.sum(row_lse) + 0.5 * jnp.sum(col_lse) - jnp.sum(jnp.diagonal(logits))) / count
    identity = jnp.eye(count, dtype=jnp.float32)
    grad_logits = GRAD_SCALE * (0.5 * jnp.exp(logits - row_lse[:, None]) + 0.5 * jnp.exp(logits - col_lse[None, :]) - identity)
    grad_spec = SCALE_LOGIT * jnp.dot(grad_logits, image_unit, precision=HIGH)
    radial = lax.optimization_barrier(jnp.sum(spectra * grad_spec, axis=-1, keepdims=True))
    grad_embed = ((grad_spec - spectra * radial) / embed_norm).astype(jnp.bfloat16)
    grad_proj = jnp.dot(pooled.T, grad_embed, preferred_element_type=jnp.float32)
    grad_pooled = jnp.dot(grad_embed, proj_weight.T, preferred_element_type=jnp.float32)
    grad_normal = jnp.broadcast_to(grad_pooled[:, None, :] / L, normal_feat.shape) * gain_float
    mean_one = lax.optimization_barrier(jnp.mean(grad_normal, axis=-1, keepdims=True))
    mean_two = lax.optimization_barrier(jnp.mean(grad_normal * normal_feat, axis=-1, keepdims=True))
    grad_resid = (inv_std * (grad_normal - mean_one - normal_feat * mean_two)).astype(jnp.bfloat16)

    def backward_one(totals, items):
        sequence, concat_rows, resid_rows = items
        acc_query, acc_key, acc_value, acc_out = totals
        queries, keys_all, values_all, attn_prob, attn_half = attend(sequence, query_weight, key_weight, value_weight)
        acc_out = acc_out + jnp.dot(concat_rows.T, resid_rows, preferred_element_type=jnp.float32)
        grad_heads = jnp.dot(resid_rows, out_weight.T, preferred_element_type=jnp.float32).astype(jnp.bfloat16)
        grad_heads = grad_heads.reshape(L, H, head_size).astype(jnp.float32)
        grad_probs = jnp.einsum('qhd,khd->hqk', grad_heads, values_all.astype(jnp.float32))
        row_dot = lax.optimization_barrier(jnp.sum(attn_prob * grad_probs, axis=-1, keepdims=True))
        grad_scores = (attn_prob * (grad_probs - row_dot) * head_size ** (-0.5)).astype(jnp.bfloat16).astype(jnp.float32)
        grad_q = jnp.einsum('hqk,khd->qhd', grad_scores, keys_all.astype(jnp.float32)).astype(jnp.bfloat16).reshape(L, D)
        grad_k = jnp.einsum('hqk,qhd->khd', grad_scores, queries.astype(jnp.float32)).astype(jnp.bfloat16).reshape(L, D)
        grad_v = jnp.einsum('hqk,qhd->khd', attn_half.astype(jnp.float32), grad_heads).astype(jnp.bfloat16).reshape(L, D)
        acc_query = acc_query + jnp.dot(sequence.T, grad_q, preferred_element_type=jnp.float32)
        acc_key = acc_key + jnp.dot(sequence.T, grad_k, preferred_element_type=jnp.float32)
        acc_value = acc_value + jnp.dot(sequence.T, grad_v, preferred_element_type=jnp.float32)
        total_input = jnp.zeros((L, D), jnp.float32)
        for group in range(N_TENSOR):
            low = group * group_cols
            high = low + group_cols
            term = jnp.dot(grad_q[:, low:high], query_weight[:, low:high].T, preferred_element_type=jnp.float32)
            term = term + jnp.dot(grad_k[:, low:high], key_weight[:, low:high].T, preferred_element_type=jnp.float32)
            term = term + jnp.dot(grad_v[:, low:high], value_weight[:, low:high].T, preferred_element_type=jnp.float32)
            total_input = total_input + term.astype(jnp.bfloat16).astype(jnp.float32)
        return ((acc_query, acc_key, acc_value, acc_out), total_input.astype(jnp.bfloat16))
    zero_square = jnp.zeros((D, D), jnp.float32)
    totals, grad_normed = lax.scan(backward_one, (zero_square, zero_square, zero_square, zero_square), (normed, head_concat, grad_resid))
    grad_query, grad_key, grad_value, grad_out = totals
    return (mean_loss, grad_normed, grad_query, grad_key, grad_value, grad_out, grad_proj)
```

```python
import jax
import jax.numpy as jnp
from jax import lax
from jax.sharding import PartitionSpec as P

D = 2048
H = 16


SCALE_LOGIT = 14.0
GRAD_SCALE = 256.0
EPSILON = 1e-05
HIGH = lax.Precision.HIGHEST


def project(inputs, weight):
    return jnp.einsum("bld,dc->blc", inputs, weight, preferred_element_type=jnp.float32).astype(
        jnp.bfloat16
    )


def split_heads(values, head_size):
    return values.reshape(values.shape[0], values.shape[1], values.shape[2] // head_size, head_size)


def chunks_rows(grad, parts):
    rows, cols = grad.shape
    return grad.reshape(parts, (rows // parts) * cols)


def chunks_cols(grad, parts):
    rows, cols = grad.shape
    return grad.reshape(rows, parts, cols // parts).transpose(1, 0, 2).reshape(parts, -1)


def local(
    stream,
    normed,
    query_weight,
    key_weight,
    value_weight,
    out_weight,
    norm_gain,
    proj_weight,
    images,
):
    seq_count = normed.shape[0]
    length = normed.shape[1]
    col_count = query_weight.shape[1]
    feat_share = stream.shape[2]
    head_size = D // H
    scale_head = head_size ** (-0.5)
    dp_parts = lax.psum(1, "dp")
    t_index = lax.axis_index("tensor")
    gain_full = lax.all_gather(norm_gain, "tensor", axis=0, tiled=True).astype(jnp.float32)
    gathered = lax.all_gather(images, "dp", axis=0, tiled=True).astype(jnp.float32)
    image_unit = gathered / jnp.sqrt(jnp.sum(gathered * gathered, axis=-1, keepdims=True) + EPSILON)

    queries = split_heads(project(normed, query_weight), head_size)
    keys_all = split_heads(project(normed, key_weight), head_size)
    values_all = split_heads(project(normed, value_weight), head_size)
    scores = (
        jnp.einsum("bqhd,bkhd->bhqk", queries, keys_all, preferred_element_type=jnp.float32)
        * scale_head
    )
    row_max = jnp.max(scores, axis=-1, keepdims=True)
    exp_scores = jnp.exp(scores - row_max)
    attn_prob = exp_scores / jnp.sum(exp_scores, axis=-1, keepdims=True)
    attn_half = attn_prob.astype(jnp.bfloat16)
    heads_out = jnp.einsum(
        "bhqk,bkhd->bqhd", attn_half, values_all, preferred_element_type=jnp.float32
    )
    head_concat = heads_out.astype(jnp.bfloat16).reshape(seq_count, length, col_count)
    partial_value = jnp.einsum(
        "blc,cd->bld", head_concat, out_weight, preferred_element_type=jnp.float32
    )
    placed_stream = lax.dynamic_update_slice_in_dim(
        jnp.zeros(partial_value.shape, jnp.float32),
        stream.astype(jnp.float32),
        t_index * feat_share,
        2,
    )
    residual = lax.psum((partial_value + placed_stream).astype(jnp.bfloat16), "tensor").astype(
        jnp.float32
    )
    center = jnp.mean(residual, axis=-1, keepdims=True)
    offset = residual - center
    variance = jnp.mean(offset * offset, axis=-1, keepdims=True)
    inv_std = lax.rsqrt(variance + EPSILON)
    normal_feat = offset * inv_std
    pooled_full = jnp.mean(normal_feat * gain_full, axis=1)
    pooled = lax.dynamic_slice_in_dim(pooled_full, t_index * feat_share, feat_share, 1).astype(
        jnp.bfloat16
    )
    embedded = lax.psum(jnp.dot(pooled, proj_weight, preferred_element_type=jnp.float32), "tensor")
    embed_norm = jnp.sqrt(jnp.sum(embedded * embedded, axis=-1, keepdims=True) + EPSILON)
    spectra = embedded / embed_norm
    logits = SCALE_LOGIT * jnp.dot(spectra, image_unit.T, precision=HIGH)
    own_start = lax.axis_index("dp") * seq_count
    columns = jnp.arange(logits.shape[1], dtype=jnp.int32)
    own_rows = own_start + jnp.arange(seq_count, dtype=jnp.int32)
    matches = (columns[None, :] == own_rows[:, None]).astype(jnp.float32)
    exp_logits = jnp.exp(logits)
    row_lse = jnp.log(jnp.sum(exp_logits, axis=1))
    diagonal = jnp.sum(logits * matches, axis=1)
    local_loss = 0.5 * jnp.sum(row_lse) - jnp.sum(diagonal)
    col_total, loss_sum = lax.psum((jnp.sum(exp_logits, axis=0), local_loss), "dp")
    col_lse = jnp.log(col_total)
    mean_loss = (loss_sum + 0.5 * jnp.sum(col_lse)) / logits.shape[1]
    grad_logits = GRAD_SCALE * (
        0.5 * jnp.exp(logits - row_lse[:, None])
        + 0.5 * jnp.exp(logits - col_lse[None, :])
        - matches
    )
    grad_spec = SCALE_LOGIT * jnp.dot(grad_logits, image_unit, precision=HIGH)
    radial = jnp.sum(spectra * grad_spec, axis=-1, keepdims=True)
    grad_embed = ((grad_spec - spectra * radial) / embed_norm).astype(jnp.bfloat16)
    grad_proj = lax.dot_general(
        pooled, grad_embed, (((0,), (0,)), ((), ())), preferred_element_type=jnp.float32
    )
    grad_pooled = lax.dot_general(
        grad_embed, proj_weight, (((1,), (1,)), ((), ())), preferred_element_type=jnp.float32
    )
    grad_pooled_full = lax.all_gather(grad_pooled, "tensor", axis=1, tiled=True)
    grad_normal = jnp.broadcast_to(
        grad_pooled_full[:, None, :] / length, normal_feat.shape
    ) * gain_full
    mean_one = jnp.mean(grad_normal, axis=-1, keepdims=True)
    mean_two = jnp.mean(grad_normal * normal_feat, axis=-1, keepdims=True)
    piece_rows = (inv_std * (grad_normal - mean_one - normal_feat * mean_two)).astype(jnp.bfloat16)
    grad_heads = jnp.einsum(
        "blw,cw->blc", piece_rows, out_weight, preferred_element_type=jnp.float32
    )
    grad_out = jnp.einsum("blc,blw->cw", head_concat, piece_rows, preferred_element_type=jnp.float32)
    grad_heads = split_heads(grad_heads.astype(jnp.bfloat16), head_size)
    grad_probs = jnp.einsum(
        "bqhd,bkhd->bhqk", grad_heads, values_all, preferred_element_type=jnp.float32
    )
    row_dot = jnp.sum(attn_prob * grad_probs, axis=-1, keepdims=True)
    grad_scores = (attn_prob * (grad_probs - row_dot) * scale_head).astype(jnp.bfloat16)
    grad_q = (
        jnp.einsum("bhqk,bkhd->bqhd", grad_scores, keys_all, preferred_element_type=jnp.float32)
        .astype(jnp.bfloat16)
        .reshape(seq_count, length, col_count)
    )
    grad_k = (
        jnp.einsum("bhqk,bqhd->bkhd", grad_scores, queries, preferred_element_type=jnp.float32)
        .astype(jnp.bfloat16)
        .reshape(seq_count, length, col_count)
    )
    grad_v = (
        jnp.einsum("bhqk,bqhd->bkhd", attn_half, grad_heads, preferred_element_type=jnp.float32)
        .astype(jnp.bfloat16)
        .reshape(seq_count, length, col_count)
    )
    back_input = jnp.einsum("blc,dc->bld", grad_q, query_weight, preferred_element_type=jnp.float32)
    back_input = back_input + jnp.einsum(
        "blc,dc->bld", grad_k, key_weight, preferred_element_type=jnp.float32
    )
    back_input = back_input + jnp.einsum(
        "blc,dc->bld", grad_v, value_weight, preferred_element_type=jnp.float32
    )
    grad_normed = lax.psum_scatter(
        back_input.astype(jnp.bfloat16), "tensor", scatter_dimension=2, tiled=True
    )
    grad_query = jnp.einsum("bld,blc->dc", normed, grad_q, preferred_element_type=jnp.float32)
    grad_key = jnp.einsum("bld,blc->dc", normed, grad_k, preferred_element_type=jnp.float32)
    grad_value = jnp.einsum("bld,blc->dc", normed, grad_v, preferred_element_type=jnp.float32)
    pieces = [
        chunks_rows(grad_query.astype(jnp.bfloat16), dp_parts),
        chunks_rows(grad_key.astype(jnp.bfloat16), dp_parts),
        chunks_rows(grad_value.astype(jnp.bfloat16), dp_parts),
        chunks_cols(grad_out.astype(jnp.bfloat16), dp_parts),
        chunks_cols(grad_proj.astype(jnp.bfloat16), dp_parts),
    ]
    widths = [piece.shape[1] for piece in pieces]
    joined = jnp.concatenate(pieces, axis=1)
    total_width = joined.shape[1]
    reduced = lax.psum_scatter(
        joined.reshape(dp_parts * 8, total_width // 8), "dp", scatter_dimension=0, tiled=True
    ).astype(jnp.float32).reshape(1, total_width)
    outs = []
    start = 0
    for width in widths:
        outs.append(reduced[0, start:start + width])
        start += width
    rows_q = D // dp_parts
    grad_query_out = outs[0].reshape(rows_q, col_count)
    grad_key_out = outs[1].reshape(rows_q, col_count)
    grad_value_out = outs[2].reshape(rows_q, col_count)
    grad_out_out = outs[3].reshape(grad_out.shape[0], grad_out.shape[1] // dp_parts)
    grad_proj_out = outs[4].reshape(grad_proj.shape[0], grad_proj.shape[1] // dp_parts)
    return (
        mean_loss,
        grad_normed,
        grad_query_out,
        grad_key_out,
        grad_value_out,
        grad_out_out,
        grad_proj_out,
    )


def solution(mesh):
    return jax.shard_map(
        local,
        mesh=mesh,
        in_specs=(
            P("dp", None, "tensor"),
            P("dp", None, None),
            P(None, "tensor"),
            P(None, "tensor"),
            P(None, "tensor"),
            P("tensor", None),
            P("tensor"),
            P("tensor", None),
            P("dp", None),
        ),
        out_specs=(
            P(),
            P("dp", None, "tensor"),
            P("dp", "tensor"),
            P("dp", "tensor"),
            P("dp", "tensor"),
            P("tensor", "dp"),
            P("tensor", "dp"),
        ),
        check_vma=False,
    )
```

```python
import jax
import jax.numpy as jnp
from jax import lax
from jax.sharding import PartitionSpec as P

D = 2048
H = 16


SCALE_LOGIT = 14.0
GRAD_SCALE = 256.0
EPSILON = 1e-05
HIGH = lax.Precision.HIGHEST


def project(inputs, weight):
    return jnp.einsum("bld,dc->blc", inputs, weight, preferred_element_type=jnp.float32).astype(
        jnp.bfloat16
    )


def split_heads(values, head_size):
    return values.reshape(values.shape[0], values.shape[1], values.shape[2] // head_size, head_size)


def chunks_rows(grad, parts):
    rows, cols = grad.shape
    return grad.reshape(parts, (rows // parts) * cols)


def chunks_cols(grad, parts):
    rows, cols = grad.shape
    return grad.reshape(rows, parts, cols // parts).transpose(1, 0, 2).reshape(parts, -1)


def xor_pairs(count, bit):
    return [(i, i ^ bit) for i in range(count)]


def tree_sum(value, axis, count):
    bit = 1
    while bit < count:
        value = value + lax.ppermute(value, axis, xor_pairs(count, bit))
        bit *= 2
    return value


def tree_gather(value, axis, count, dim):
    index = lax.axis_index(axis)
    bit = 1
    while bit < count:
        other = lax.ppermute(value, axis, xor_pairs(count, bit))
        low = (index // bit) % 2 == 0
        value = jnp.where(
            low,
            jnp.concatenate([value, other], dim),
            jnp.concatenate([other, value], dim),
        )
        bit *= 2
    return value


def tree_scatter(buffer, axis, count):
    index = lax.axis_index(axis)
    total = None
    bit = 1
    step = 0
    while bit < count:
        rows = buffer.shape[0]
        halves = buffer.reshape(rows // 2, 2, buffer.shape[1])
        own = (index // bit) % 2
        keep = lax.dynamic_index_in_dim(halves, own, axis=1, keepdims=False)
        send = lax.dynamic_index_in_dim(halves, 1 - own, axis=1, keepdims=False)
        received = lax.ppermute(send.astype(jnp.bfloat16), axis, xor_pairs(count, bit))
        buffer = keep.astype(jnp.float32) + received.astype(jnp.float32)
        bit *= 2
        step += 1
    return buffer


def local(
    stream,
    normed,
    query_weight,
    key_weight,
    value_weight,
    out_weight,
    norm_gain,
    proj_weight,
    images,
):
    seq_count = normed.shape[0]
    length = normed.shape[1]
    col_count = query_weight.shape[1]
    feat_share = stream.shape[2]
    head_size = D // H
    scale_head = head_size ** (-0.5)
    dp_parts = lax.psum(1, "dp")
    t_parts = lax.psum(1, "tensor")
    t_index = lax.axis_index("tensor")
    gain_full = tree_gather(norm_gain, "tensor", t_parts, 0).astype(jnp.float32)
    gathered = tree_gather(images, "dp", dp_parts, 0).astype(jnp.float32)
    image_unit = gathered / jnp.sqrt(jnp.sum(gathered * gathered, axis=-1, keepdims=True) + EPSILON)

    queries = split_heads(project(normed, query_weight), head_size)
    keys_all = split_heads(project(normed, key_weight), head_size)
    values_all = split_heads(project(normed, value_weight), head_size)
    scores = (
        jnp.einsum("bqhd,bkhd->bhqk", queries, keys_all, preferred_element_type=jnp.float32)
        * scale_head
    )
    row_max = jnp.max(scores, axis=-1, keepdims=True)
    exp_scores = jnp.exp(scores - row_max)
    attn_prob = exp_scores / jnp.sum(exp_scores, axis=-1, keepdims=True)
    attn_half = attn_prob.astype(jnp.bfloat16)
    heads_out = jnp.einsum(
        "bhqk,bkhd->bqhd", attn_half, values_all, preferred_element_type=jnp.float32
    )
    head_concat = heads_out.astype(jnp.bfloat16).reshape(seq_count, length, col_count)
    partial_value = jnp.einsum(
        "blc,cd->bld", head_concat, out_weight, preferred_element_type=jnp.float32
    )
    placed_stream = lax.dynamic_update_slice_in_dim(
        jnp.zeros(partial_value.shape, jnp.float32),
        stream.astype(jnp.float32),
        t_index * feat_share,
        2,
    )
    residual = lax.psum((partial_value + placed_stream).astype(jnp.bfloat16), "tensor").astype(
        jnp.float32
    )
    center = jnp.mean(residual, axis=-1, keepdims=True)
    offset = residual - center
    variance = jnp.mean(offset * offset, axis=-1, keepdims=True)
    inv_std = lax.rsqrt(variance + EPSILON)
    normal_feat = offset * inv_std
    pooled_full = jnp.mean(normal_feat * gain_full, axis=1)
    pooled = lax.dynamic_slice_in_dim(pooled_full, t_index * feat_share, feat_share, 1).astype(
        jnp.bfloat16
    )
    embedded = tree_sum(
        jnp.dot(pooled, proj_weight, preferred_element_type=jnp.float32), "tensor", t_parts
    )
    embed_norm = jnp.sqrt(jnp.sum(embedded * embedded, axis=-1, keepdims=True) + EPSILON)
    spectra = embedded / embed_norm
    logits = SCALE_LOGIT * jnp.dot(spectra, image_unit.T, precision=HIGH)
    own_start = lax.axis_index("dp") * seq_count
    columns = jnp.arange(logits.shape[1], dtype=jnp.int32)
    own_rows = own_start + jnp.arange(seq_count, dtype=jnp.int32)
    matches = (columns[None, :] == own_rows[:, None]).astype(jnp.float32)
    exp_logits = jnp.exp(logits)
    row_lse = jnp.log(jnp.sum(exp_logits, axis=1))
    diagonal = jnp.sum(logits * matches, axis=1)
    local_loss = 0.5 * jnp.sum(row_lse) - jnp.sum(diagonal)
    loss_terms = tree_sum(
        jnp.concatenate([jnp.sum(exp_logits, axis=0), local_loss[None]]), "dp", dp_parts
    )
    col_total = loss_terms[:-1]
    loss_sum = loss_terms[-1]
    col_lse = jnp.log(col_total)
    mean_loss = (loss_sum + 0.5 * jnp.sum(col_lse)) / logits.shape[1]
    grad_logits = GRAD_SCALE * (
        0.5 * jnp.exp(logits - row_lse[:, None])
        + 0.5 * jnp.exp(logits - col_lse[None, :])
        - matches
    )
    grad_spec = SCALE_LOGIT * jnp.dot(grad_logits, image_unit, precision=HIGH)
    radial = jnp.sum(spectra * grad_spec, axis=-1, keepdims=True)
    grad_embed = ((grad_spec - spectra * radial) / embed_norm).astype(jnp.bfloat16)
    grad_proj = lax.dot_general(
        pooled, grad_embed, (((0,), (0,)), ((), ())), preferred_element_type=jnp.float32
    )
    grad_pooled = lax.dot_general(
        grad_embed, proj_weight, (((1,), (1,)), ((), ())), preferred_element_type=jnp.float32
    )
    grad_pooled_full = tree_gather(grad_pooled, "tensor", t_parts, 1)
    grad_normal = jnp.broadcast_to(
        grad_pooled_full[:, None, :] / length, normal_feat.shape
    ) * gain_full
    mean_one = jnp.mean(grad_normal, axis=-1, keepdims=True)
    mean_two = jnp.mean(grad_normal * normal_feat, axis=-1, keepdims=True)
    piece_rows = (inv_std * (grad_normal - mean_one - normal_feat * mean_two)).astype(jnp.bfloat16)
    grad_heads = jnp.einsum(
        "blw,cw->blc", piece_rows, out_weight, preferred_element_type=jnp.float32
    )
    grad_out = jnp.einsum("blc,blw->cw", head_concat, piece_rows, preferred_element_type=jnp.float32)
    grad_heads = split_heads(grad_heads.astype(jnp.bfloat16), head_size)
    grad_probs = jnp.einsum(
        "bqhd,bkhd->bhqk", grad_heads, values_all, preferred_element_type=jnp.float32
    )
    row_dot = jnp.sum(attn_prob * grad_probs, axis=-1, keepdims=True)
    grad_scores = (attn_prob * (grad_probs - row_dot) * scale_head).astype(jnp.bfloat16)
    grad_q = (
        jnp.einsum("bhqk,bkhd->bqhd", grad_scores, keys_all, preferred_element_type=jnp.float32)
        .astype(jnp.bfloat16)
        .reshape(seq_count, length, col_count)
    )
    grad_k = (
        jnp.einsum("bhqk,bqhd->bkhd", grad_scores, queries, preferred_element_type=jnp.float32)
        .astype(jnp.bfloat16)
        .reshape(seq_count, length, col_count)
    )
    grad_v = (
        jnp.einsum("bhqk,bqhd->bkhd", attn_half, grad_heads, preferred_element_type=jnp.float32)
        .astype(jnp.bfloat16)
        .reshape(seq_count, length, col_count)
    )
    back_input = jnp.einsum("blc,dc->bld", grad_q, query_weight, preferred_element_type=jnp.float32)
    back_input = back_input + jnp.einsum(
        "blc,dc->bld", grad_k, key_weight, preferred_element_type=jnp.float32
    )
    back_input = back_input + jnp.einsum(
        "blc,dc->bld", grad_v, value_weight, preferred_element_type=jnp.float32
    )
    grad_normed = lax.psum_scatter(
        back_input.astype(jnp.bfloat16), "tensor", scatter_dimension=2, tiled=True
    )
    grad_query = jnp.einsum("bld,blc->dc", normed, grad_q, preferred_element_type=jnp.float32)
    grad_key = jnp.einsum("bld,blc->dc", normed, grad_k, preferred_element_type=jnp.float32)
    grad_value = jnp.einsum("bld,blc->dc", normed, grad_v, preferred_element_type=jnp.float32)
    pieces = [
        chunks_rows(grad_query.astype(jnp.bfloat16), dp_parts),
        chunks_rows(grad_key.astype(jnp.bfloat16), dp_parts),
        chunks_rows(grad_value.astype(jnp.bfloat16), dp_parts),
        chunks_cols(grad_out.astype(jnp.bfloat16), dp_parts),
        chunks_cols(grad_proj.astype(jnp.bfloat16), dp_parts),
    ]
    widths = [piece.shape[1] for piece in pieces]
    reduced = tree_scatter(jnp.concatenate(pieces, axis=1), "dp", dp_parts)
    outs = []
    start = 0
    for width in widths:
        outs.append(reduced[0, start:start + width])
        start += width
    rows_q = D // dp_parts
    grad_query_out = outs[0].reshape(rows_q, col_count)
    grad_key_out = outs[1].reshape(rows_q, col_count)
    grad_value_out = outs[2].reshape(rows_q, col_count)
    grad_out_out = outs[3].reshape(grad_out.shape[0], grad_out.shape[1] // dp_parts)
    grad_proj_out = outs[4].reshape(grad_proj.shape[0], grad_proj.shape[1] // dp_parts)
    return (
        mean_loss,
        grad_normed,
        grad_query_out,
        grad_key_out,
        grad_value_out,
        grad_out_out,
        grad_proj_out,
    )


def solution(mesh):
    return jax.shard_map(
        local,
        mesh=mesh,
        in_specs=(
            P("dp", None, "tensor"),
            P("dp", None, None),
            P(None, "tensor"),
            P(None, "tensor"),
            P(None, "tensor"),
            P("tensor", None),
            P("tensor"),
            P("tensor", None),
            P("dp", None),
        ),
        out_specs=(
            P(),
            P("dp", None, "tensor"),
            P("dp", "tensor"),
            P("dp", "tensor"),
            P("dp", "tensor"),
            P("tensor", "dp"),
            P("tensor", "dp"),
        ),
        check_vma=False,
    )
```

```python
import jax
import jax.numpy as jnp
from jax import lax
from jax.sharding import PartitionSpec as P

D = 2048
H = 16


SCALE_LOGIT = 14.0
GRAD_SCALE = 256.0
EPSILON = 1e-05
HIGH = lax.Precision.HIGHEST


def project(inputs, weight):
    return jnp.einsum("bld,dc->blc", inputs, weight, preferred_element_type=jnp.float32).astype(
        jnp.bfloat16
    )


def split_heads(values, head_size):
    return values.reshape(values.shape[0], values.shape[1], values.shape[2] // head_size, head_size)


def chunks_rows(grad, parts):
    rows, cols = grad.shape
    return grad.reshape(parts, (rows // parts) * cols)


def chunks_cols(grad, parts):
    rows, cols = grad.shape
    return grad.reshape(rows, parts, cols // parts).transpose(1, 0, 2).reshape(parts, -1)


def xor_pairs(count, bit):
    return [(i, i ^ bit) for i in range(count)]


def tree_sum(value, axis, count):
    bit = 1
    while bit < count:
        value = value + lax.ppermute(value, axis, xor_pairs(count, bit))
        bit *= 2
    return value


def tree_gather(value, axis, count, dim):
    index = lax.axis_index(axis)
    bit = 1
    while bit < count:
        other = lax.ppermute(value, axis, xor_pairs(count, bit))
        low = (index // bit) % 2 == 0
        value = jnp.where(
            low,
            jnp.concatenate([value, other], dim),
            jnp.concatenate([other, value], dim),
        )
        bit *= 2
    return value


def tree_scatter(buffer, axis, count):
    index = lax.axis_index(axis)
    while buffer.shape[0] > 1:
        rows = buffer.shape[0]
        bit = rows // 2
        halves = buffer.reshape(2, bit, buffer.shape[1])
        own = (index // bit) % 2
        keep = lax.dynamic_index_in_dim(halves, own, axis=0, keepdims=False)
        send = lax.dynamic_index_in_dim(halves, 1 - own, axis=0, keepdims=False)
        received = lax.ppermute(send.astype(jnp.bfloat16), axis, xor_pairs(count, bit))
        buffer = keep.astype(jnp.float32) + received.astype(jnp.float32)
    return buffer


def local(
    stream,
    normed,
    query_weight,
    key_weight,
    value_weight,
    out_weight,
    norm_gain,
    proj_weight,
    images,
):
    seq_count = normed.shape[0]
    length = normed.shape[1]
    col_count = query_weight.shape[1]
    feat_share = stream.shape[2]
    head_size = D // H
    scale_head = head_size ** (-0.5)
    dp_parts = lax.psum(1, "dp")
    t_parts = lax.psum(1, "tensor")
    t_index = lax.axis_index("tensor")
    gain_full = tree_gather(norm_gain, "tensor", t_parts, 0).astype(jnp.float32)
    gathered = tree_gather(images, "dp", dp_parts, 0).astype(jnp.float32)
    image_unit = gathered / jnp.sqrt(jnp.sum(gathered * gathered, axis=-1, keepdims=True) + EPSILON)

    queries = split_heads(project(normed, query_weight), head_size)
    keys_all = split_heads(project(normed, key_weight), head_size)
    values_all = split_heads(project(normed, value_weight), head_size)
    scores = (
        jnp.einsum("bqhd,bkhd->bhqk", queries, keys_all, preferred_element_type=jnp.float32)
        * scale_head
    )
    row_max = jnp.max(scores, axis=-1, keepdims=True)
    exp_scores = jnp.exp(scores - row_max)
    attn_prob = exp_scores / jnp.sum(exp_scores, axis=-1, keepdims=True)
    attn_half = attn_prob.astype(jnp.bfloat16)
    heads_out = jnp.einsum(
        "bhqk,bkhd->bqhd", attn_half, values_all, preferred_element_type=jnp.float32
    )
    head_concat = heads_out.astype(jnp.bfloat16).reshape(seq_count, length, col_count)
    partial_value = jnp.einsum(
        "blc,cd->bld", head_concat, out_weight, preferred_element_type=jnp.float32
    )
    placed_stream = lax.dynamic_update_slice_in_dim(
        jnp.zeros(partial_value.shape, jnp.float32),
        stream.astype(jnp.float32),
        t_index * feat_share,
        2,
    )
    residual = lax.psum((partial_value + placed_stream).astype(jnp.bfloat16), "tensor").astype(
        jnp.float32
    )
    center = jnp.mean(residual, axis=-1, keepdims=True)
    offset = residual - center
    variance = jnp.mean(offset * offset, axis=-1, keepdims=True)
    inv_std = lax.rsqrt(variance + EPSILON)
    normal_feat = offset * inv_std
    pooled_full = jnp.mean(normal_feat * gain_full, axis=1)
    pooled = lax.dynamic_slice_in_dim(pooled_full, t_index * feat_share, feat_share, 1).astype(
        jnp.bfloat16
    )
    embedded = tree_sum(
        jnp.dot(pooled, proj_weight, preferred_element_type=jnp.float32), "tensor", t_parts
    )
    embed_norm = jnp.sqrt(jnp.sum(embedded * embedded, axis=-1, keepdims=True) + EPSILON)
    spectra = embedded / embed_norm
    logits = SCALE_LOGIT * jnp.dot(spectra, image_unit.T, precision=HIGH)
    own_start = lax.axis_index("dp") * seq_count
    columns = jnp.arange(logits.shape[1], dtype=jnp.int32)
    own_rows = own_start + jnp.arange(seq_count, dtype=jnp.int32)
    matches = (columns[None, :] == own_rows[:, None]).astype(jnp.float32)
    exp_logits = jnp.exp(logits)
    row_lse = jnp.log(jnp.sum(exp_logits, axis=1))
    diagonal = jnp.sum(logits * matches, axis=1)
    local_loss = 0.5 * jnp.sum(row_lse) - jnp.sum(diagonal)
    loss_terms = tree_sum(
        jnp.concatenate([jnp.sum(exp_logits, axis=0), local_loss[None]]), "dp", dp_parts
    )
    col_total = loss_terms[:-1]
    loss_sum = loss_terms[-1]
    col_lse = jnp.log(col_total)
    mean_loss = (loss_sum + 0.5 * jnp.sum(col_lse)) / logits.shape[1]
    grad_logits = GRAD_SCALE * (
        0.5 * jnp.exp(logits - row_lse[:, None])
        + 0.5 * jnp.exp(logits - col_lse[None, :])
        - matches
    )
    grad_spec = SCALE_LOGIT * jnp.dot(grad_logits, image_unit, precision=HIGH)
    radial = jnp.sum(spectra * grad_spec, axis=-1, keepdims=True)
    grad_embed = ((grad_spec - spectra * radial) / embed_norm).astype(jnp.bfloat16)
    grad_proj = lax.dot_general(
        pooled, grad_embed, (((0,), (0,)), ((), ())), preferred_element_type=jnp.float32
    )
    grad_pooled = lax.dot_general(
        grad_embed, proj_weight, (((1,), (1,)), ((), ())), preferred_element_type=jnp.float32
    )
    grad_pooled_full = tree_gather(grad_pooled, "tensor", t_parts, 1)
    grad_normal = jnp.broadcast_to(
        grad_pooled_full[:, None, :] / length, normal_feat.shape
    ) * gain_full
    mean_one = jnp.mean(grad_normal, axis=-1, keepdims=True)
    mean_two = jnp.mean(grad_normal * normal_feat, axis=-1, keepdims=True)
    piece_rows = (inv_std * (grad_normal - mean_one - normal_feat * mean_two)).astype(jnp.bfloat16)
    grad_heads = jnp.einsum(
        "blw,cw->blc", piece_rows, out_weight, preferred_element_type=jnp.float32
    )
    grad_out = jnp.einsum("blc,blw->cw", head_concat, piece_rows, preferred_element_type=jnp.float32)
    grad_heads = split_heads(grad_heads.astype(jnp.bfloat16), head_size)
    grad_probs = jnp.einsum(
        "bqhd,bkhd->bhqk", grad_heads, values_all, preferred_element_type=jnp.float32
    )
    row_dot = jnp.sum(attn_prob * grad_probs, axis=-1, keepdims=True)
    grad_scores = (attn_prob * (grad_probs - row_dot) * scale_head).astype(jnp.bfloat16)
    grad_q = (
        jnp.einsum("bhqk,bkhd->bqhd", grad_scores, keys_all, preferred_element_type=jnp.float32)
        .astype(jnp.bfloat16)
        .reshape(seq_count, length, col_count)
    )
    grad_k = (
        jnp.einsum("bhqk,bqhd->bkhd", grad_scores, queries, preferred_element_type=jnp.float32)
        .astype(jnp.bfloat16)
        .reshape(seq_count, length, col_count)
    )
    grad_v = (
        jnp.einsum("bhqk,bqhd->bkhd", attn_half, grad_heads, preferred_element_type=jnp.float32)
        .astype(jnp.bfloat16)
        .reshape(seq_count, length, col_count)
    )
    back_input = jnp.einsum("blc,dc->bld", grad_q, query_weight, preferred_element_type=jnp.float32)
    back_input = back_input + jnp.einsum(
        "blc,dc->bld", grad_k, key_weight, preferred_element_type=jnp.float32
    )
    back_input = back_input + jnp.einsum(
        "blc,dc->bld", grad_v, value_weight, preferred_element_type=jnp.float32
    )
    late_pieces = [
        chunks_cols(grad_out.astype(jnp.bfloat16), dp_parts),
        chunks_cols(grad_proj.astype(jnp.bfloat16), dp_parts),
    ]
    late_reduced = tree_scatter(jnp.concatenate(late_pieces, axis=1), "dp", dp_parts)
    grad_query = jnp.einsum("bld,blc->dc", normed, grad_q, preferred_element_type=jnp.float32)
    grad_key = jnp.einsum("bld,blc->dc", normed, grad_k, preferred_element_type=jnp.float32)
    grad_value = jnp.einsum("bld,blc->dc", normed, grad_v, preferred_element_type=jnp.float32)
    early_pieces = [
        chunks_rows(grad_query.astype(jnp.bfloat16), dp_parts),
        chunks_rows(grad_key.astype(jnp.bfloat16), dp_parts),
        chunks_rows(grad_value.astype(jnp.bfloat16), dp_parts),
    ]
    back_half, early_joined = lax.optimization_barrier(
        (back_input.astype(jnp.bfloat16), jnp.concatenate(early_pieces, axis=1))
    )
    grad_normed = lax.psum_scatter(back_half, "tensor", scatter_dimension=2, tiled=True)
    early_reduced = tree_scatter(early_joined, "dp", dp_parts)
    widths = [piece.shape[1] for piece in early_pieces + late_pieces]
    reduced = jnp.concatenate([early_reduced, late_reduced], axis=1)
    outs = []
    start = 0
    for width in widths:
        outs.append(reduced[0, start:start + width])
        start += width
    rows_q = D // dp_parts
    grad_query_out = outs[0].reshape(rows_q, col_count)
    grad_key_out = outs[1].reshape(rows_q, col_count)
    grad_value_out = outs[2].reshape(rows_q, col_count)
    grad_out_out = outs[3].reshape(grad_out.shape[0], grad_out.shape[1] // dp_parts)
    grad_proj_out = outs[4].reshape(grad_proj.shape[0], grad_proj.shape[1] // dp_parts)
    return (
        mean_loss,
        grad_normed,
        grad_query_out,
        grad_key_out,
        grad_value_out,
        grad_out_out,
        grad_proj_out,
    )


def solution(mesh):
    return jax.shard_map(
        local,
        mesh=mesh,
        in_specs=(
            P("dp", None, "tensor"),
            P("dp", None, None),
            P(None, "tensor"),
            P(None, "tensor"),
            P(None, "tensor"),
            P("tensor", None),
            P("tensor"),
            P("tensor", None),
            P("dp", None),
        ),
        out_specs=(
            P(),
            P("dp", None, "tensor"),
            P("dp", "tensor"),
            P("dp", "tensor"),
            P("dp", "tensor"),
            P("tensor", "dp"),
            P("tensor", "dp"),
        ),
        check_vma=False,
    )
```

```python
import jax
import jax.numpy as jnp
from jax import lax
from jax.sharding import PartitionSpec as P

D = 2048
H = 16


SCALE_LOGIT = 14.0
GRAD_SCALE = 256.0
EPSILON = 1e-05
HIGH = lax.Precision.HIGHEST


def project(inputs, weight):
    return jnp.einsum("bld,dc->blc", inputs, weight, preferred_element_type=jnp.float32).astype(
        jnp.bfloat16
    )


def split_heads(values, head_size):
    return values.reshape(values.shape[0], values.shape[1], values.shape[2] // head_size, head_size)


def chunks_rows(grad, parts):
    rows, cols = grad.shape
    return grad.reshape(parts, (rows // parts) * cols)


def chunks_cols(grad, parts):
    rows, cols = grad.shape
    return grad.reshape(rows, parts, cols // parts).transpose(1, 0, 2).reshape(parts, -1)


def xor_pairs(count, bit):
    return [(i, i ^ bit) for i in range(count)]


def tree_sum(value, axis, count):
    bit = 1
    while bit < count:
        value = value + lax.ppermute(value, axis, xor_pairs(count, bit))
        bit *= 2
    return value


def tree_gather(value, axis, count, dim):
    index = lax.axis_index(axis)
    bit = 1
    while bit < count:
        other = lax.ppermute(value, axis, xor_pairs(count, bit))
        low = (index // bit) % 2 == 0
        value = jnp.where(
            low,
            jnp.concatenate([value, other], dim),
            jnp.concatenate([other, value], dim),
        )
        bit *= 2
    return value


def tree_scatter(buffer, axis, count, order):
    index = lax.axis_index(axis)
    width = buffer.shape[1]
    levels = len(order)
    cube = buffer.reshape((2,) * levels + (width,))
    natural = [count // (2 ** (k + 1)) for k in range(levels)]
    cube = cube.transpose([natural.index(bit) for bit in order] + [levels])
    buffer = cube.reshape(count, width)
    for bit in order:
        rows = buffer.shape[0]
        halves = buffer.reshape(2, rows // 2, width)
        own = (index // bit) % 2
        keep = lax.dynamic_index_in_dim(halves, own, axis=0, keepdims=False)
        send = lax.dynamic_index_in_dim(halves, 1 - own, axis=0, keepdims=False)
        received = lax.ppermute(send.astype(jnp.bfloat16), axis, xor_pairs(count, bit))
        buffer = keep.astype(jnp.float32) + received.astype(jnp.float32)
    return buffer


def halving_order(count):
    bits = [2 ** k for k in range(count.bit_length() - 1)]
    if count == 32:
        return [1, 8, 2, 16, 4]
    return bits


def local(
    stream,
    normed,
    query_weight,
    key_weight,
    value_weight,
    out_weight,
    norm_gain,
    proj_weight,
    images,
):
    seq_count = normed.shape[0]
    length = normed.shape[1]
    col_count = query_weight.shape[1]
    feat_share = stream.shape[2]
    head_size = D // H
    scale_head = head_size ** (-0.5)
    dp_parts = lax.psum(1, "dp")
    t_parts = lax.psum(1, "tensor")
    t_index = lax.axis_index("tensor")
    gain_full = tree_gather(norm_gain, "tensor", t_parts, 0).astype(jnp.float32)
    gathered = tree_gather(images, "dp", dp_parts, 0).astype(jnp.float32)
    image_unit = gathered / jnp.sqrt(jnp.sum(gathered * gathered, axis=-1, keepdims=True) + EPSILON)

    queries = split_heads(project(normed, query_weight), head_size)
    keys_all = split_heads(project(normed, key_weight), head_size)
    values_all = split_heads(project(normed, value_weight), head_size)
    scores = (
        jnp.einsum("bqhd,bkhd->bhqk", queries, keys_all, preferred_element_type=jnp.float32)
        * scale_head
    )
    row_max = jnp.max(scores, axis=-1, keepdims=True)
    exp_scores = jnp.exp(scores - row_max)
    attn_prob = exp_scores / jnp.sum(exp_scores, axis=-1, keepdims=True)
    attn_half = attn_prob.astype(jnp.bfloat16)
    heads_out = jnp.einsum(
        "bhqk,bkhd->bqhd", attn_half, values_all, preferred_element_type=jnp.float32
    )
    head_concat = heads_out.astype(jnp.bfloat16).reshape(seq_count, length, col_count)
    partial_value = jnp.einsum(
        "blc,cd->bld", head_concat, out_weight, preferred_element_type=jnp.float32
    )
    blocks = (
        partial_value.astype(jnp.bfloat16)
        .reshape(seq_count, length, t_parts, feat_share)
        .transpose(2, 0, 1, 3)
    )
    arrived = lax.all_to_all(blocks, "tensor", 0, 0, tiled=True)
    own_residual = stream.astype(jnp.float32) + jnp.sum(arrived.astype(jnp.float32), axis=0)
    spread = jnp.broadcast_to(
        own_residual.astype(jnp.bfloat16)[None], (t_parts,) + own_residual.shape
    )
    collected = lax.all_to_all(spread, "tensor", 0, 0, tiled=True)
    residual = (
        collected.transpose(1, 2, 0, 3).reshape(seq_count, length, t_parts * feat_share)
    ).astype(jnp.float32)
    center = jnp.mean(residual, axis=-1, keepdims=True)
    offset = residual - center
    variance = jnp.mean(offset * offset, axis=-1, keepdims=True)
    inv_std = lax.rsqrt(variance + EPSILON)
    normal_feat = offset * inv_std
    pooled_full = jnp.mean(normal_feat * gain_full, axis=1)
    pooled = lax.dynamic_slice_in_dim(pooled_full, t_index * feat_share, feat_share, 1).astype(
        jnp.bfloat16
    )
    embedded = tree_sum(
        jnp.dot(pooled, proj_weight, preferred_element_type=jnp.float32), "tensor", t_parts
    )
    embed_norm = jnp.sqrt(jnp.sum(embedded * embedded, axis=-1, keepdims=True) + EPSILON)
    spectra = embedded / embed_norm
    logits = SCALE_LOGIT * jnp.dot(spectra, image_unit.T, precision=HIGH)
    own_start = lax.axis_index("dp") * seq_count
    columns = jnp.arange(logits.shape[1], dtype=jnp.int32)
    own_rows = own_start + jnp.arange(seq_count, dtype=jnp.int32)
    matches = (columns[None, :] == own_rows[:, None]).astype(jnp.float32)
    exp_logits = jnp.exp(logits)
    row_lse = jnp.log(jnp.sum(exp_logits, axis=1))
    diagonal = jnp.sum(logits * matches, axis=1)
    local_loss = 0.5 * jnp.sum(row_lse) - jnp.sum(diagonal)
    loss_terms = tree_sum(
        jnp.concatenate([jnp.sum(exp_logits, axis=0), local_loss[None]]), "dp", dp_parts
    )
    col_total = loss_terms[:-1]
    loss_sum = loss_terms[-1]
    col_lse = jnp.log(col_total)
    mean_loss = (loss_sum + 0.5 * jnp.sum(col_lse)) / logits.shape[1]
    grad_logits = GRAD_SCALE * (
        0.5 * jnp.exp(logits - row_lse[:, None])
        + 0.5 * jnp.exp(logits - col_lse[None, :])
        - matches
    )
    grad_spec = SCALE_LOGIT * jnp.dot(grad_logits, image_unit, precision=HIGH)
    radial = jnp.sum(spectra * grad_spec, axis=-1, keepdims=True)
    grad_embed = ((grad_spec - spectra * radial) / embed_norm).astype(jnp.bfloat16)
    grad_proj = lax.dot_general(
        pooled, grad_embed, (((0,), (0,)), ((), ())), preferred_element_type=jnp.float32
    )
    grad_pooled = lax.dot_general(
        grad_embed, proj_weight, (((1,), (1,)), ((), ())), preferred_element_type=jnp.float32
    )
    grad_pooled_full = tree_gather(grad_pooled, "tensor", t_parts, 1)
    grad_normal = jnp.broadcast_to(
        grad_pooled_full[:, None, :] / length, normal_feat.shape
    ) * gain_full
    mean_one = jnp.mean(grad_normal, axis=-1, keepdims=True)
    mean_two = jnp.mean(grad_normal * normal_feat, axis=-1, keepdims=True)
    piece_rows = (inv_std * (grad_normal - mean_one - normal_feat * mean_two)).astype(jnp.bfloat16)
    grad_heads = jnp.einsum(
        "blw,cw->blc", piece_rows, out_weight, preferred_element_type=jnp.float32
    )
    grad_out = jnp.einsum("blc,blw->cw", head_concat, piece_rows, preferred_element_type=jnp.float32)
    grad_heads = split_heads(grad_heads.astype(jnp.bfloat16), head_size)
    grad_probs = jnp.einsum(
        "bqhd,bkhd->bhqk", grad_heads, values_all, preferred_element_type=jnp.float32
    )
    row_dot = jnp.sum(attn_prob * grad_probs, axis=-1, keepdims=True)
    grad_scores = (attn_prob * (grad_probs - row_dot) * scale_head).astype(jnp.bfloat16)
    grad_q = (
        jnp.einsum("bhqk,bkhd->bqhd", grad_scores, keys_all, preferred_element_type=jnp.float32)
        .astype(jnp.bfloat16)
        .reshape(seq_count, length, col_count)
    )
    grad_k = (
        jnp.einsum("bhqk,bqhd->bkhd", grad_scores, queries, preferred_element_type=jnp.float32)
        .astype(jnp.bfloat16)
        .reshape(seq_count, length, col_count)
    )
    grad_v = (
        jnp.einsum("bhqk,bqhd->bkhd", attn_half, grad_heads, preferred_element_type=jnp.float32)
        .astype(jnp.bfloat16)
        .reshape(seq_count, length, col_count)
    )
    back_input = jnp.einsum("blc,dc->bld", grad_q, query_weight, preferred_element_type=jnp.float32)
    back_input = back_input + jnp.einsum(
        "blc,dc->bld", grad_k, key_weight, preferred_element_type=jnp.float32
    )
    back_input = back_input + jnp.einsum(
        "blc,dc->bld", grad_v, value_weight, preferred_element_type=jnp.float32
    )
    late_pieces = [
        chunks_cols(grad_out.astype(jnp.bfloat16), dp_parts),
        chunks_cols(grad_proj.astype(jnp.bfloat16), dp_parts),
    ]
    late_reduced = tree_scatter(jnp.concatenate(late_pieces, axis=1), "dp", dp_parts, halving_order(dp_parts))
    grad_query = jnp.einsum("bld,blc->dc", normed, grad_q, preferred_element_type=jnp.float32)
    grad_key = jnp.einsum("bld,blc->dc", normed, grad_k, preferred_element_type=jnp.float32)
    grad_value = jnp.einsum("bld,blc->dc", normed, grad_v, preferred_element_type=jnp.float32)
    early_pieces = [
        chunks_rows(grad_query.astype(jnp.bfloat16), dp_parts),
        chunks_rows(grad_key.astype(jnp.bfloat16), dp_parts),
        chunks_rows(grad_value.astype(jnp.bfloat16), dp_parts),
    ]
    back_half, early_joined = lax.optimization_barrier(
        (back_input.astype(jnp.bfloat16), jnp.concatenate(early_pieces, axis=1))
    )
    grad_normed = lax.psum_scatter(back_half, "tensor", scatter_dimension=2, tiled=True)
    early_reduced = tree_scatter(early_joined, "dp", dp_parts, halving_order(dp_parts))
    widths = [piece.shape[1] for piece in early_pieces + late_pieces]
    reduced = jnp.concatenate([early_reduced, late_reduced], axis=1)
    outs = []
    start = 0
    for width in widths:
        outs.append(reduced[0, start:start + width])
        start += width
    rows_q = D // dp_parts
    grad_query_out = outs[0].reshape(rows_q, col_count)
    grad_key_out = outs[1].reshape(rows_q, col_count)
    grad_value_out = outs[2].reshape(rows_q, col_count)
    grad_out_out = outs[3].reshape(grad_out.shape[0], grad_out.shape[1] // dp_parts)
    grad_proj_out = outs[4].reshape(grad_proj.shape[0], grad_proj.shape[1] // dp_parts)
    return (
        mean_loss,
        grad_normed,
        grad_query_out,
        grad_key_out,
        grad_value_out,
        grad_out_out,
        grad_proj_out,
    )


def solution(mesh):
    return jax.shard_map(
        local,
        mesh=mesh,
        in_specs=(
            P("dp", None, "tensor"),
            P("dp", None, None),
            P(None, "tensor"),
            P(None, "tensor"),
            P(None, "tensor"),
            P("tensor", None),
            P("tensor"),
            P("tensor", None),
            P("dp", None),
        ),
        out_specs=(
            P(),
            P("dp", None, "tensor"),
            P("dp", "tensor"),
            P("dp", "tensor"),
            P("dp", "tensor"),
            P("tensor", "dp"),
            P("tensor", "dp"),
        ),
        check_vma=False,
    )
```

```python
import jax
import jax.numpy as jnp
from jax import lax
from jax.sharding import PartitionSpec as P

D = 2048
H = 16


SCALE_LOGIT = 14.0
GRAD_SCALE = 256.0
EPSILON = 1e-05
HIGH = lax.Precision.HIGHEST


def project(inputs, weight):
    return jnp.einsum("bld,dc->blc", inputs, weight, preferred_element_type=jnp.float32).astype(
        jnp.bfloat16
    )


def split_heads(values, head_size):
    return values.reshape(values.shape[0], values.shape[1], values.shape[2] // head_size, head_size)


def chunks_rows(grad, parts):
    rows, cols = grad.shape
    return grad.reshape(parts, (rows // parts) * cols)


def chunks_cols(grad, parts):
    rows, cols = grad.shape
    return grad.reshape(rows, parts, cols // parts).transpose(1, 0, 2).reshape(parts, -1)


def xor_pairs(count, bit):
    return [(i, i ^ bit) for i in range(count)]


def tree_sum(value, axis, count):
    bit = 1
    while bit < count:
        value = value + lax.ppermute(value, axis, xor_pairs(count, bit))
        bit *= 2
    return value


def tree_gather(value, axis, count, dim):
    index = lax.axis_index(axis)
    bit = 1
    while bit < count:
        other = lax.ppermute(value, axis, xor_pairs(count, bit))
        low = (index // bit) % 2 == 0
        value = jnp.where(
            low,
            jnp.concatenate([value, other], dim),
            jnp.concatenate([other, value], dim),
        )
        bit *= 2
    return value


def tree_scatter(buffer, axis, count, order):
    index = lax.axis_index(axis)
    width = buffer.shape[1]
    levels = len(order)
    cube = buffer.reshape((2,) * levels + (width,))
    natural = [count // (2 ** (k + 1)) for k in range(levels)]
    cube = cube.transpose([natural.index(bit) for bit in order] + [levels])
    buffer = cube.reshape(count, width)
    for bit in order:
        rows = buffer.shape[0]
        halves = buffer.reshape(2, rows // 2, width)
        own = (index // bit) % 2
        keep = lax.dynamic_index_in_dim(halves, own, axis=0, keepdims=False)
        send = lax.dynamic_index_in_dim(halves, 1 - own, axis=0, keepdims=False)
        received = lax.ppermute(send.astype(jnp.bfloat16), axis, xor_pairs(count, bit))
        buffer = keep.astype(jnp.float32) + received.astype(jnp.float32)
    return buffer


def halving_order(count):
    return [count // (2 ** (k + 1)) for k in range(count.bit_length() - 1)]


def local(
    stream,
    normed,
    query_weight,
    key_weight,
    value_weight,
    out_weight,
    norm_gain,
    proj_weight,
    images,
):
    seq_count = normed.shape[0]
    length = normed.shape[1]
    col_count = query_weight.shape[1]
    feat_share = stream.shape[2]
    head_size = D // H
    scale_head = head_size ** (-0.5)
    dp_parts = lax.psum(1, "dp")
    t_parts = lax.psum(1, "tensor")
    t_index = lax.axis_index("tensor")
    gain_full = tree_gather(norm_gain, "tensor", t_parts, 0).astype(jnp.float32)
    gathered = tree_gather(images, "dp", dp_parts, 0).astype(jnp.float32)
    image_unit = gathered / jnp.sqrt(jnp.sum(gathered * gathered, axis=-1, keepdims=True) + EPSILON)

    queries = split_heads(project(normed, query_weight), head_size)
    keys_all = split_heads(project(normed, key_weight), head_size)
    values_all = split_heads(project(normed, value_weight), head_size)
    scores = (
        jnp.einsum("bqhd,bkhd->bhqk", queries, keys_all, preferred_element_type=jnp.float32)
        * scale_head
    )
    row_max = jnp.max(scores, axis=-1, keepdims=True)
    exp_scores = jnp.exp(scores - row_max)
    attn_prob = exp_scores / jnp.sum(exp_scores, axis=-1, keepdims=True)
    attn_half = attn_prob.astype(jnp.bfloat16)
    heads_out = jnp.einsum(
        "bhqk,bkhd->bqhd", attn_half, values_all, preferred_element_type=jnp.float32
    )
    head_concat = heads_out.astype(jnp.bfloat16).reshape(seq_count, length, col_count)
    partial_value = jnp.einsum(
        "blc,cd->bld", head_concat, out_weight, preferred_element_type=jnp.float32
    )
    blocks = partial_value.astype(jnp.bfloat16).reshape(seq_count, length, t_parts, feat_share)
    arrived = lax.all_to_all(blocks, "tensor", 2, 2, tiled=True)
    own_residual = stream.astype(jnp.float32) + jnp.sum(arrived.astype(jnp.float32), axis=2)
    spread = jnp.broadcast_to(
        own_residual.astype(jnp.bfloat16)[:, :, None, :],
        (seq_count, length, t_parts, feat_share),
    )
    collected = lax.all_to_all(spread, "tensor", 2, 2, tiled=True)
    residual = collected.reshape(seq_count, length, t_parts * feat_share).astype(jnp.float32)
    center = jnp.mean(residual, axis=-1, keepdims=True)
    offset = residual - center
    variance = jnp.mean(offset * offset, axis=-1, keepdims=True)
    inv_std = lax.rsqrt(variance + EPSILON)
    normal_feat = offset * inv_std
    pooled_full = jnp.mean(normal_feat * gain_full, axis=1)
    pooled = lax.dynamic_slice_in_dim(pooled_full, t_index * feat_share, feat_share, 1).astype(
        jnp.bfloat16
    )
    embedded = tree_sum(
        jnp.dot(pooled, proj_weight, preferred_element_type=jnp.float32), "tensor", t_parts
    )
    embed_norm = jnp.sqrt(jnp.sum(embedded * embedded, axis=-1, keepdims=True) + EPSILON)
    spectra = embedded / embed_norm
    logits = SCALE_LOGIT * jnp.dot(spectra, image_unit.T, precision=HIGH)
    own_start = lax.axis_index("dp") * seq_count
    columns = jnp.arange(logits.shape[1], dtype=jnp.int32)
    own_rows = own_start + jnp.arange(seq_count, dtype=jnp.int32)
    matches = (columns[None, :] == own_rows[:, None]).astype(jnp.float32)
    exp_logits = jnp.exp(logits)
    row_lse = jnp.log(jnp.sum(exp_logits, axis=1))
    diagonal = jnp.sum(logits * matches, axis=1)
    local_loss = 0.5 * jnp.sum(row_lse) - jnp.sum(diagonal)
    loss_terms = tree_sum(
        jnp.concatenate([jnp.sum(exp_logits, axis=0), local_loss[None]]), "dp", dp_parts
    )
    col_total = loss_terms[:-1]
    loss_sum = loss_terms[-1]
    col_lse = jnp.log(col_total)
    mean_loss = (loss_sum + 0.5 * jnp.sum(col_lse)) / logits.shape[1]
    grad_logits = GRAD_SCALE * (
        0.5 * jnp.exp(logits - row_lse[:, None])
        + 0.5 * jnp.exp(logits - col_lse[None, :])
        - matches
    )
    grad_spec = SCALE_LOGIT * jnp.dot(grad_logits, image_unit, precision=HIGH)
    radial = jnp.sum(spectra * grad_spec, axis=-1, keepdims=True)
    grad_embed = ((grad_spec - spectra * radial) / embed_norm).astype(jnp.bfloat16)
    grad_proj = lax.dot_general(
        pooled, grad_embed, (((0,), (0,)), ((), ())), preferred_element_type=jnp.float32
    )
    grad_pooled = lax.dot_general(
        grad_embed, proj_weight, (((1,), (1,)), ((), ())), preferred_element_type=jnp.float32
    )
    grad_pooled_full = tree_gather(grad_pooled, "tensor", t_parts, 1)
    grad_normal = jnp.broadcast_to(
        grad_pooled_full[:, None, :] / length, normal_feat.shape
    ) * gain_full
    mean_one = jnp.mean(grad_normal, axis=-1, keepdims=True)
    mean_two = jnp.mean(grad_normal * normal_feat, axis=-1, keepdims=True)
    piece_rows = (inv_std * (grad_normal - mean_one - normal_feat * mean_two)).astype(jnp.bfloat16)
    grad_heads = jnp.einsum(
        "blw,cw->blc", piece_rows, out_weight, preferred_element_type=jnp.float32
    )
    grad_out = jnp.einsum("blc,blw->cw", head_concat, piece_rows, preferred_element_type=jnp.float32)
    grad_heads = split_heads(grad_heads.astype(jnp.bfloat16), head_size)
    grad_probs = jnp.einsum(
        "bqhd,bkhd->bhqk", grad_heads, values_all, preferred_element_type=jnp.float32
    )
    row_dot = jnp.sum(attn_prob * grad_probs, axis=-1, keepdims=True)
    grad_scores = (attn_prob * (grad_probs - row_dot) * scale_head).astype(jnp.bfloat16)
    grad_q = (
        jnp.einsum("bhqk,bkhd->bqhd", grad_scores, keys_all, preferred_element_type=jnp.float32)
        .astype(jnp.bfloat16)
        .reshape(seq_count, length, col_count)
    )
    grad_k = (
        jnp.einsum("bhqk,bqhd->bkhd", grad_scores, queries, preferred_element_type=jnp.float32)
        .astype(jnp.bfloat16)
        .reshape(seq_count, length, col_count)
    )
    grad_v = (
        jnp.einsum("bhqk,bqhd->bkhd", attn_half, grad_heads, preferred_element_type=jnp.float32)
        .astype(jnp.bfloat16)
        .reshape(seq_count, length, col_count)
    )
    back_input = jnp.einsum("blc,dc->bld", grad_q, query_weight, preferred_element_type=jnp.float32)
    back_input = back_input + jnp.einsum(
        "blc,dc->bld", grad_k, key_weight, preferred_element_type=jnp.float32
    )
    back_input = back_input + jnp.einsum(
        "blc,dc->bld", grad_v, value_weight, preferred_element_type=jnp.float32
    )
    late_pieces = [
        chunks_cols(grad_out.astype(jnp.bfloat16), dp_parts),
        chunks_cols(grad_proj.astype(jnp.bfloat16), dp_parts),
    ]
    late_reduced = tree_scatter(jnp.concatenate(late_pieces, axis=1), "dp", dp_parts, halving_order(dp_parts))
    grad_query = jnp.einsum("bld,blc->dc", normed, grad_q, preferred_element_type=jnp.float32)
    grad_key = jnp.einsum("bld,blc->dc", normed, grad_k, preferred_element_type=jnp.float32)
    grad_value = jnp.einsum("bld,blc->dc", normed, grad_v, preferred_element_type=jnp.float32)
    early_pieces = [
        chunks_rows(grad_query.astype(jnp.bfloat16), dp_parts),
        chunks_rows(grad_key.astype(jnp.bfloat16), dp_parts),
        chunks_rows(grad_value.astype(jnp.bfloat16), dp_parts),
    ]
    back_half, early_joined = lax.optimization_barrier(
        (back_input.astype(jnp.bfloat16), jnp.concatenate(early_pieces, axis=1))
    )
    grad_normed = lax.psum_scatter(back_half, "tensor", scatter_dimension=2, tiled=True)
    early_reduced = tree_scatter(early_joined, "dp", dp_parts, halving_order(dp_parts))
    widths = [piece.shape[1] for piece in early_pieces + late_pieces]
    reduced = jnp.concatenate([early_reduced, late_reduced], axis=1)
    outs = []
    start = 0
    for width in widths:
        outs.append(reduced[0, start:start + width])
        start += width
    rows_q = D // dp_parts
    grad_query_out = outs[0].reshape(rows_q, col_count)
    grad_key_out = outs[1].reshape(rows_q, col_count)
    grad_value_out = outs[2].reshape(rows_q, col_count)
    grad_out_out = outs[3].reshape(grad_out.shape[0], grad_out.shape[1] // dp_parts)
    grad_proj_out = outs[4].reshape(grad_proj.shape[0], grad_proj.shape[1] // dp_parts)
    return (
        mean_loss,
        grad_normed,
        grad_query_out,
        grad_key_out,
        grad_value_out,
        grad_out_out,
        grad_proj_out,
    )


def solution(mesh):
    return jax.shard_map(
        local,
        mesh=mesh,
        in_specs=(
            P("dp", None, "tensor"),
            P("dp", None, None),
            P(None, "tensor"),
            P(None, "tensor"),
            P(None, "tensor"),
            P("tensor", None),
            P("tensor"),
            P("tensor", None),
            P("dp", None),
        ),
        out_specs=(
            P(),
            P("dp", None, "tensor"),
            P("dp", "tensor"),
            P("dp", "tensor"),
            P("dp", "tensor"),
            P("tensor", "dp"),
            P("tensor", "dp"),
        ),
        check_vma=False,
    )
```

```python
import jax
import jax.numpy as jnp
from jax import lax
from jax.sharding import PartitionSpec as P

D = 2048
H = 16


SCALE_LOGIT = 14.0
GRAD_SCALE = 256.0
EPSILON = 1e-05
HIGH = lax.Precision.HIGHEST


def project(inputs, weight):
    return jnp.einsum("bld,dc->blc", inputs, weight, preferred_element_type=jnp.float32).astype(
        jnp.bfloat16
    )


def split_heads(values, head_size):
    return values.reshape(values.shape[0], values.shape[1], values.shape[2] // head_size, head_size)


def chunks_rows(grad, parts):
    rows, cols = grad.shape
    return grad.reshape(parts, (rows // parts) * cols)


def chunks_cols(grad, parts):
    rows, cols = grad.shape
    return grad.reshape(rows, parts, cols // parts).transpose(1, 0, 2).reshape(parts, -1)


def xor_pairs(count, bit):
    return [(i, i ^ bit) for i in range(count)]


def tree_sum(value, axis, count):
    bit = 1
    while bit < count:
        value = value + lax.ppermute(value, axis, xor_pairs(count, bit))
        bit *= 2
    return value


def tree_gather(value, axis, count, dim):
    index = lax.axis_index(axis)
    bit = 1
    while bit < count:
        other = lax.ppermute(value, axis, xor_pairs(count, bit))
        low = (index // bit) % 2 == 0
        value = jnp.where(
            low,
            jnp.concatenate([value, other], dim),
            jnp.concatenate([other, value], dim),
        )
        bit *= 2
    return value


def tree_scatter(buffer, axis, count, order):
    index = lax.axis_index(axis)
    width = buffer.shape[1]
    levels = len(order)
    cube = buffer.reshape((2,) * levels + (width,))
    natural = [count // (2 ** (k + 1)) for k in range(levels)]
    cube = cube.transpose([natural.index(bit) for bit in order] + [levels])
    buffer = cube.reshape(count, width)
    for bit in order:
        rows = buffer.shape[0]
        halves = buffer.reshape(2, rows // 2, width)
        own = (index // bit) % 2
        keep = lax.dynamic_index_in_dim(halves, own, axis=0, keepdims=False)
        send = lax.dynamic_index_in_dim(halves, 1 - own, axis=0, keepdims=False)
        received = lax.ppermute(send.astype(jnp.bfloat16), axis, xor_pairs(count, bit))
        buffer = keep.astype(jnp.float32) + received.astype(jnp.float32)
    return buffer


def halving_order(count):
    return [count // (2 ** (k + 1)) for k in range(count.bit_length() - 1)]


def local(
    stream,
    normed,
    query_weight,
    key_weight,
    value_weight,
    out_weight,
    norm_gain,
    proj_weight,
    images,
):
    seq_count = normed.shape[0]
    length = normed.shape[1]
    col_count = query_weight.shape[1]
    feat_share = stream.shape[2]
    head_size = D // H
    scale_head = head_size ** (-0.5)
    dp_parts = lax.psum(1, "dp")
    t_parts = lax.psum(1, "tensor")
    t_index = lax.axis_index("tensor")
    gain_full = tree_gather(norm_gain, "tensor", t_parts, 0).astype(jnp.float32)
    gathered = tree_gather(images, "dp", dp_parts, 0).astype(jnp.float32)
    image_unit = gathered / jnp.sqrt(jnp.sum(gathered * gathered, axis=-1, keepdims=True) + EPSILON)

    queries = split_heads(project(normed, query_weight), head_size)
    keys_all = split_heads(project(normed, key_weight), head_size)
    values_all = split_heads(project(normed, value_weight), head_size)
    scores = (
        jnp.einsum("bqhd,bkhd->bhqk", queries, keys_all, preferred_element_type=jnp.float32)
        * scale_head
    )
    row_max = jnp.max(scores, axis=-1, keepdims=True)
    exp_scores = jnp.exp(scores - row_max)
    attn_prob = exp_scores / jnp.sum(exp_scores, axis=-1, keepdims=True)
    attn_half = attn_prob.astype(jnp.bfloat16)
    heads_out = jnp.einsum(
        "bhqk,bkhd->bqhd", attn_half, values_all, preferred_element_type=jnp.float32
    )
    head_concat = heads_out.astype(jnp.bfloat16).reshape(seq_count, length, col_count)
    partial_value = jnp.einsum(
        "blc,cd->bld", head_concat, out_weight, preferred_element_type=jnp.float32
    )
    blocks = partial_value.astype(jnp.bfloat16).reshape(seq_count, length, t_parts, feat_share)
    arrived = lax.all_to_all(blocks, "tensor", 2, 2, tiled=True)
    own_residual = stream.astype(jnp.float32) + jnp.sum(arrived.astype(jnp.float32), axis=2)
    residual = lax.all_gather(
        own_residual.astype(jnp.bfloat16), "tensor", axis=2, tiled=True
    ).astype(jnp.float32)
    center = jnp.mean(residual, axis=-1, keepdims=True)
    offset = residual - center
    variance = jnp.mean(offset * offset, axis=-1, keepdims=True)
    inv_std = lax.rsqrt(variance + EPSILON)
    normal_feat = offset * inv_std
    pooled_full = jnp.mean(normal_feat * gain_full, axis=1)
    pooled = lax.dynamic_slice_in_dim(pooled_full, t_index * feat_share, feat_share, 1).astype(
        jnp.bfloat16
    )
    embedded = tree_sum(
        jnp.dot(pooled, proj_weight, preferred_element_type=jnp.float32), "tensor", t_parts
    )
    embed_norm = jnp.sqrt(jnp.sum(embedded * embedded, axis=-1, keepdims=True) + EPSILON)
    spectra = embedded / embed_norm
    logits = SCALE_LOGIT * jnp.dot(spectra, image_unit.T, precision=HIGH)
    own_start = lax.axis_index("dp") * seq_count
    columns = jnp.arange(logits.shape[1], dtype=jnp.int32)
    own_rows = own_start + jnp.arange(seq_count, dtype=jnp.int32)
    matches = (columns[None, :] == own_rows[:, None]).astype(jnp.float32)
    exp_logits = jnp.exp(logits)
    row_lse = jnp.log(jnp.sum(exp_logits, axis=1))
    diagonal = jnp.sum(logits * matches, axis=1)
    local_loss = 0.5 * jnp.sum(row_lse) - jnp.sum(diagonal)
    loss_terms = tree_sum(
        jnp.concatenate([jnp.sum(exp_logits, axis=0), local_loss[None]]), "dp", dp_parts
    )
    col_total = loss_terms[:-1]
    loss_sum = loss_terms[-1]
    col_lse = jnp.log(col_total)
    mean_loss = (loss_sum + 0.5 * jnp.sum(col_lse)) / logits.shape[1]
    grad_logits = GRAD_SCALE * (
        0.5 * jnp.exp(logits - row_lse[:, None])
        + 0.5 * jnp.exp(logits - col_lse[None, :])
        - matches
    )
    grad_spec = SCALE_LOGIT * jnp.dot(grad_logits, image_unit, precision=HIGH)
    radial = jnp.sum(spectra * grad_spec, axis=-1, keepdims=True)
    grad_embed = ((grad_spec - spectra * radial) / embed_norm).astype(jnp.bfloat16)
    grad_proj = lax.dot_general(
        pooled, grad_embed, (((0,), (0,)), ((), ())), preferred_element_type=jnp.float32
    )
    grad_pooled = lax.dot_general(
        grad_embed, proj_weight, (((1,), (1,)), ((), ())), preferred_element_type=jnp.float32
    )
    grad_pooled_full = tree_gather(grad_pooled, "tensor", t_parts, 1)
    grad_normal = jnp.broadcast_to(
        grad_pooled_full[:, None, :] / length, normal_feat.shape
    ) * gain_full
    mean_one = jnp.mean(grad_normal, axis=-1, keepdims=True)
    mean_two = jnp.mean(grad_normal * normal_feat, axis=-1, keepdims=True)
    piece_rows = (inv_std * (grad_normal - mean_one - normal_feat * mean_two)).astype(jnp.bfloat16)
    grad_heads = jnp.einsum(
        "blw,cw->blc", piece_rows, out_weight, preferred_element_type=jnp.float32
    )
    grad_out = jnp.einsum("blc,blw->cw", head_concat, piece_rows, preferred_element_type=jnp.float32)
    grad_heads = split_heads(grad_heads.astype(jnp.bfloat16), head_size)
    grad_probs = jnp.einsum(
        "bqhd,bkhd->bhqk", grad_heads, values_all, preferred_element_type=jnp.float32
    )
    row_dot = jnp.sum(attn_prob * grad_probs, axis=-1, keepdims=True)
    grad_scores = (attn_prob * (grad_probs - row_dot) * scale_head).astype(jnp.bfloat16)
    grad_q = (
        jnp.einsum("bhqk,bkhd->bqhd", grad_scores, keys_all, preferred_element_type=jnp.float32)
        .astype(jnp.bfloat16)
        .reshape(seq_count, length, col_count)
    )
    grad_k = (
        jnp.einsum("bhqk,bqhd->bkhd", grad_scores, queries, preferred_element_type=jnp.float32)
        .astype(jnp.bfloat16)
        .reshape(seq_count, length, col_count)
    )
    grad_v = (
        jnp.einsum("bhqk,bqhd->bkhd", attn_half, grad_heads, preferred_element_type=jnp.float32)
        .astype(jnp.bfloat16)
        .reshape(seq_count, length, col_count)
    )
    back_input = jnp.einsum("blc,dc->bld", grad_q, query_weight, preferred_element_type=jnp.float32)
    back_input = back_input + jnp.einsum(
        "blc,dc->bld", grad_k, key_weight, preferred_element_type=jnp.float32
    )
    back_input = back_input + jnp.einsum(
        "blc,dc->bld", grad_v, value_weight, preferred_element_type=jnp.float32
    )
    late_pieces = [
        chunks_cols(grad_out.astype(jnp.bfloat16), dp_parts),
        chunks_cols(grad_proj.astype(jnp.bfloat16), dp_parts),
    ]
    late_reduced = tree_scatter(jnp.concatenate(late_pieces, axis=1), "dp", dp_parts, halving_order(dp_parts))
    grad_query = jnp.einsum("bld,blc->dc", normed, grad_q, preferred_element_type=jnp.float32)
    grad_key = jnp.einsum("bld,blc->dc", normed, grad_k, preferred_element_type=jnp.float32)
    grad_value = jnp.einsum("bld,blc->dc", normed, grad_v, preferred_element_type=jnp.float32)
    early_pieces = [
        chunks_rows(grad_query.astype(jnp.bfloat16), dp_parts),
        chunks_rows(grad_key.astype(jnp.bfloat16), dp_parts),
        chunks_rows(grad_value.astype(jnp.bfloat16), dp_parts),
    ]
    back_half, early_joined = lax.optimization_barrier(
        (back_input.astype(jnp.bfloat16), jnp.concatenate(early_pieces, axis=1))
    )
    grad_normed = lax.psum_scatter(back_half, "tensor", scatter_dimension=2, tiled=True)
    early_reduced = tree_scatter(early_joined, "dp", dp_parts, halving_order(dp_parts))
    widths = [piece.shape[1] for piece in early_pieces + late_pieces]
    reduced = jnp.concatenate([early_reduced, late_reduced], axis=1)
    outs = []
    start = 0
    for width in widths:
        outs.append(reduced[0, start:start + width])
        start += width
    rows_q = D // dp_parts
    grad_query_out = outs[0].reshape(rows_q, col_count)
    grad_key_out = outs[1].reshape(rows_q, col_count)
    grad_value_out = outs[2].reshape(rows_q, col_count)
    grad_out_out = outs[3].reshape(grad_out.shape[0], grad_out.shape[1] // dp_parts)
    grad_proj_out = outs[4].reshape(grad_proj.shape[0], grad_proj.shape[1] // dp_parts)
    return (
        mean_loss,
        grad_normed,
        grad_query_out,
        grad_key_out,
        grad_value_out,
        grad_out_out,
        grad_proj_out,
    )


def solution(mesh):
    return jax.shard_map(
        local,
        mesh=mesh,
        in_specs=(
            P("dp", None, "tensor"),
            P("dp", None, None),
            P(None, "tensor"),
            P(None, "tensor"),
            P(None, "tensor"),
            P("tensor", None),
            P("tensor"),
            P("tensor", None),
            P("dp", None),
        ),
        out_specs=(
            P(),
            P("dp", None, "tensor"),
            P("dp", "tensor"),
            P("dp", "tensor"),
            P("dp", "tensor"),
            P("tensor", "dp"),
            P("tensor", "dp"),
        ),
        check_vma=False,
    )
```

```python
import jax
import jax.numpy as jnp
from jax import lax
from jax.sharding import PartitionSpec as P

D = 2048
H = 16


SCALE_LOGIT = 14.0
GRAD_SCALE = 256.0
EPSILON = 1e-05
HIGH = lax.Precision.HIGHEST


def project(inputs, weight):
    return jnp.einsum("bld,dc->blc", inputs, weight, preferred_element_type=jnp.float32).astype(
        jnp.bfloat16
    )


def split_heads(values, head_size):
    return values.reshape(values.shape[0], values.shape[1], values.shape[2] // head_size, head_size)


def chunks_rows(grad, parts):
    rows, cols = grad.shape
    return grad.reshape(parts, (rows // parts) * cols)


def chunks_cols(grad, parts):
    rows, cols = grad.shape
    return grad.reshape(rows, parts, cols // parts).transpose(1, 0, 2).reshape(parts, -1)


def xor_pairs(count, bit):
    return [(i, i ^ bit) for i in range(count)]


def tree_sum(value, axis, count):
    bit = 1
    while bit < count:
        value = value + lax.ppermute(value, axis, xor_pairs(count, bit))
        bit *= 2
    return value


def tree_gather(value, axis, count, dim):
    index = lax.axis_index(axis)
    bit = 1
    while bit < count:
        other = lax.ppermute(value, axis, xor_pairs(count, bit))
        low = (index // bit) % 2 == 0
        value = jnp.where(
            low,
            jnp.concatenate([value, other], dim),
            jnp.concatenate([other, value], dim),
        )
        bit *= 2
    return value


def bit_axes(count, order):
    natural = [count // (2 ** (k + 1)) for k in range(len(order))]
    return [natural.index(bit) for bit in order]


def tree_scatter(buffer, axis, count, order, arranged=False):
    index = lax.axis_index(axis)
    width = buffer.shape[1]
    levels = len(order)
    if not arranged:
        cube = buffer.reshape((2,) * levels + (width,))
        cube = cube.transpose(bit_axes(count, order) + [levels])
        buffer = cube.reshape(count, width)
    for bit in order:
        rows = buffer.shape[0]
        halves = buffer.reshape(2, rows // 2, width)
        own = (index // bit) % 2
        keep = lax.dynamic_index_in_dim(halves, own, axis=0, keepdims=False)
        send = lax.dynamic_index_in_dim(halves, 1 - own, axis=0, keepdims=False)
        received = lax.ppermute(send.astype(jnp.bfloat16), axis, xor_pairs(count, bit))
        buffer = keep.astype(jnp.float32) + received.astype(jnp.float32)
    return buffer


def halving_order(count):
    return [count // (2 ** (k + 1)) for k in range(count.bit_length() - 1)]


def route_order(count):
    if count == 32:
        return [1, 8, 2, 16, 4]
    return halving_order(count)


def local(
    stream,
    normed,
    query_weight,
    key_weight,
    value_weight,
    out_weight,
    norm_gain,
    proj_weight,
    images,
):
    seq_count = normed.shape[0]
    length = normed.shape[1]
    col_count = query_weight.shape[1]
    feat_share = stream.shape[2]
    head_size = D // H
    scale_head = head_size ** (-0.5)
    dp_parts = lax.psum(1, "dp")
    t_parts = lax.psum(1, "tensor")
    t_index = lax.axis_index("tensor")
    gain_full = tree_gather(norm_gain, "tensor", t_parts, 0).astype(jnp.float32)
    gathered = tree_gather(images, "dp", dp_parts, 0).astype(jnp.float32)
    image_unit = gathered / jnp.sqrt(jnp.sum(gathered * gathered, axis=-1, keepdims=True) + EPSILON)

    queries = split_heads(project(normed, query_weight), head_size)
    keys_all = split_heads(project(normed, key_weight), head_size)
    values_all = split_heads(project(normed, value_weight), head_size)
    scores = (
        jnp.einsum("bqhd,bkhd->bhqk", queries, keys_all, preferred_element_type=jnp.float32)
        * scale_head
    )
    row_max = jnp.max(scores, axis=-1, keepdims=True)
    exp_scores = jnp.exp(scores - row_max)
    attn_prob = exp_scores / jnp.sum(exp_scores, axis=-1, keepdims=True)
    attn_half = attn_prob.astype(jnp.bfloat16)
    heads_out = jnp.einsum(
        "bhqk,bkhd->bqhd", attn_half, values_all, preferred_element_type=jnp.float32
    )
    head_concat = heads_out.astype(jnp.bfloat16).reshape(seq_count, length, col_count)
    partial_value = jnp.einsum(
        "blc,cd->bld", head_concat, out_weight, preferred_element_type=jnp.float32
    )
    blocks = partial_value.astype(jnp.bfloat16).reshape(seq_count, length, t_parts, feat_share)
    arrived = lax.all_to_all(blocks, "tensor", 2, 2, tiled=True)
    own_residual = stream.astype(jnp.float32) + jnp.sum(arrived.astype(jnp.float32), axis=2)
    residual = lax.all_gather(
        own_residual.astype(jnp.bfloat16), "tensor", axis=2, tiled=True
    ).astype(jnp.float32)
    order = route_order(dp_parts)
    levels = len(order)
    block = D // dp_parts
    normed_cube = normed.reshape((seq_count, length) + (2,) * levels + (block,))
    normed_arranged = normed_cube.transpose(
        [0, 1] + [2 + axis_id for axis_id in bit_axes(dp_parts, order)] + [2 + levels]
    ).reshape(seq_count, length, D)
    residual, normed_arranged = lax.optimization_barrier((residual, normed_arranged))
    center = jnp.mean(residual, axis=-1, keepdims=True)
    offset = residual - center
    variance = jnp.mean(offset * offset, axis=-1, keepdims=True)
    inv_std = lax.rsqrt(variance + EPSILON)
    normal_feat = offset * inv_std
    pooled_full = jnp.mean(normal_feat * gain_full, axis=1)
    pooled = lax.dynamic_slice_in_dim(pooled_full, t_index * feat_share, feat_share, 1).astype(
        jnp.bfloat16
    )
    embedded = tree_sum(
        jnp.dot(pooled, proj_weight, preferred_element_type=jnp.float32), "tensor", t_parts
    )
    embed_norm = jnp.sqrt(jnp.sum(embedded * embedded, axis=-1, keepdims=True) + EPSILON)
    spectra = embedded / embed_norm
    logits = SCALE_LOGIT * jnp.dot(spectra, image_unit.T, precision=HIGH)
    own_start = lax.axis_index("dp") * seq_count
    columns = jnp.arange(logits.shape[1], dtype=jnp.int32)
    own_rows = own_start + jnp.arange(seq_count, dtype=jnp.int32)
    matches = (columns[None, :] == own_rows[:, None]).astype(jnp.float32)
    exp_logits = jnp.exp(logits)
    row_lse = jnp.log(jnp.sum(exp_logits, axis=1))
    diagonal = jnp.sum(logits * matches, axis=1)
    local_loss = 0.5 * jnp.sum(row_lse) - jnp.sum(diagonal)
    loss_terms = tree_sum(
        jnp.concatenate([jnp.sum(exp_logits, axis=0), local_loss[None]]), "dp", dp_parts
    )
    col_total = loss_terms[:-1]
    loss_sum = loss_terms[-1]
    col_lse = jnp.log(col_total)
    mean_loss = (loss_sum + 0.5 * jnp.sum(col_lse)) / logits.shape[1]
    grad_logits = GRAD_SCALE * (
        0.5 * jnp.exp(logits - row_lse[:, None])
        + 0.5 * jnp.exp(logits - col_lse[None, :])
        - matches
    )
    grad_spec = SCALE_LOGIT * jnp.dot(grad_logits, image_unit, precision=HIGH)
    radial = jnp.sum(spectra * grad_spec, axis=-1, keepdims=True)
    grad_embed = ((grad_spec - spectra * radial) / embed_norm).astype(jnp.bfloat16)
    grad_proj = lax.dot_general(
        pooled, grad_embed, (((0,), (0,)), ((), ())), preferred_element_type=jnp.float32
    )
    grad_pooled = lax.dot_general(
        grad_embed, proj_weight, (((1,), (1,)), ((), ())), preferred_element_type=jnp.float32
    )
    grad_pooled_full = tree_gather(grad_pooled, "tensor", t_parts, 1)
    grad_normal = jnp.broadcast_to(
        grad_pooled_full[:, None, :] / length, normal_feat.shape
    ) * gain_full
    mean_one = jnp.mean(grad_normal, axis=-1, keepdims=True)
    mean_two = jnp.mean(grad_normal * normal_feat, axis=-1, keepdims=True)
    piece_rows = (inv_std * (grad_normal - mean_one - normal_feat * mean_two)).astype(jnp.bfloat16)
    grad_heads = jnp.einsum(
        "blw,cw->blc", piece_rows, out_weight, preferred_element_type=jnp.float32
    )
    grad_out = jnp.einsum("blc,blw->cw", head_concat, piece_rows, preferred_element_type=jnp.float32)
    grad_heads = split_heads(grad_heads.astype(jnp.bfloat16), head_size)
    grad_probs = jnp.einsum(
        "bqhd,bkhd->bhqk", grad_heads, values_all, preferred_element_type=jnp.float32
    )
    row_dot = jnp.sum(attn_prob * grad_probs, axis=-1, keepdims=True)
    grad_scores = (attn_prob * (grad_probs - row_dot) * scale_head).astype(jnp.bfloat16)
    grad_q = (
        jnp.einsum("bhqk,bkhd->bqhd", grad_scores, keys_all, preferred_element_type=jnp.float32)
        .astype(jnp.bfloat16)
        .reshape(seq_count, length, col_count)
    )
    grad_k = (
        jnp.einsum("bhqk,bqhd->bkhd", grad_scores, queries, preferred_element_type=jnp.float32)
        .astype(jnp.bfloat16)
        .reshape(seq_count, length, col_count)
    )
    grad_v = (
        jnp.einsum("bhqk,bqhd->bkhd", attn_half, grad_heads, preferred_element_type=jnp.float32)
        .astype(jnp.bfloat16)
        .reshape(seq_count, length, col_count)
    )
    back_input = jnp.einsum("blc,dc->bld", grad_q, query_weight, preferred_element_type=jnp.float32)
    back_input = back_input + jnp.einsum(
        "blc,dc->bld", grad_k, key_weight, preferred_element_type=jnp.float32
    )
    back_input = back_input + jnp.einsum(
        "blc,dc->bld", grad_v, value_weight, preferred_element_type=jnp.float32
    )
    late_pieces = [
        chunks_cols(grad_out.astype(jnp.bfloat16), dp_parts),
        chunks_cols(grad_proj.astype(jnp.bfloat16), dp_parts),
    ]
    late_reduced = tree_scatter(jnp.concatenate(late_pieces, axis=1), "dp", dp_parts, halving_order(dp_parts))
    grad_query = jnp.einsum(
        "bld,blc->dc", normed_arranged, grad_q, preferred_element_type=jnp.float32
    )
    grad_key = jnp.einsum("bld,blc->dc", normed_arranged, grad_k, preferred_element_type=jnp.float32)
    grad_value = jnp.einsum(
        "bld,blc->dc", normed_arranged, grad_v, preferred_element_type=jnp.float32
    )
    early_pieces = [
        chunks_rows(grad_query.astype(jnp.bfloat16), dp_parts),
        chunks_rows(grad_key.astype(jnp.bfloat16), dp_parts),
        chunks_rows(grad_value.astype(jnp.bfloat16), dp_parts),
    ]
    back_half, early_joined = lax.optimization_barrier(
        (back_input.astype(jnp.bfloat16), jnp.concatenate(early_pieces, axis=1))
    )
    grad_normed = lax.psum_scatter(back_half, "tensor", scatter_dimension=2, tiled=True)
    early_reduced = tree_scatter(early_joined, "dp", dp_parts, order, arranged=True)
    widths = [piece.shape[1] for piece in early_pieces + late_pieces]
    reduced = jnp.concatenate([early_reduced, late_reduced], axis=1)
    outs = []
    start = 0
    for width in widths:
        outs.append(reduced[0, start:start + width])
        start += width
    rows_q = D // dp_parts
    grad_query_out = outs[0].reshape(rows_q, col_count)
    grad_key_out = outs[1].reshape(rows_q, col_count)
    grad_value_out = outs[2].reshape(rows_q, col_count)
    grad_out_out = outs[3].reshape(grad_out.shape[0], grad_out.shape[1] // dp_parts)
    grad_proj_out = outs[4].reshape(grad_proj.shape[0], grad_proj.shape[1] // dp_parts)
    return (
        mean_loss,
        grad_normed,
        grad_query_out,
        grad_key_out,
        grad_value_out,
        grad_out_out,
        grad_proj_out,
    )


def solution(mesh):
    return jax.shard_map(
        local,
        mesh=mesh,
        in_specs=(
            P("dp", None, "tensor"),
            P("dp", None, None),
            P(None, "tensor"),
            P(None, "tensor"),
            P(None, "tensor"),
            P("tensor", None),
            P("tensor"),
            P("tensor", None),
            P("dp", None),
        ),
        out_specs=(
            P(),
            P("dp", None, "tensor"),
            P("dp", "tensor"),
            P("dp", "tensor"),
            P("dp", "tensor"),
            P("tensor", "dp"),
            P("tensor", "dp"),
        ),
        check_vma=False,
    )
```

```python
import jax
import jax.numpy as jnp
from jax import lax
from jax.sharding import PartitionSpec as P

D = 2048
H = 16


SCALE_LOGIT = 14.0
GRAD_SCALE = 256.0
EPSILON = 1e-05
HIGH = lax.Precision.HIGHEST


def project(inputs, weight):
    return jnp.einsum("bld,dc->blc", inputs, weight, preferred_element_type=jnp.float32).astype(
        jnp.bfloat16
    )


def split_heads(values, head_size):
    return values.reshape(values.shape[0], values.shape[1], values.shape[2] // head_size, head_size)


def chunks_rows(grad, parts):
    rows, cols = grad.shape
    return grad.reshape(parts, (rows // parts) * cols)


def chunks_cols(grad, parts):
    rows, cols = grad.shape
    return grad.reshape(rows, parts, cols // parts).transpose(1, 0, 2).reshape(parts, -1)


def xor_pairs(count, bit):
    return [(i, i ^ bit) for i in range(count)]


def tree_sum(value, axis, count):
    bit = 1
    while bit < count:
        value = value + lax.ppermute(value, axis, xor_pairs(count, bit))
        bit *= 2
    return value


def tree_gather(value, axis, count, dim):
    index = lax.axis_index(axis)
    bit = 1
    while bit < count:
        other = lax.ppermute(value, axis, xor_pairs(count, bit))
        low = (index // bit) % 2 == 0
        value = jnp.where(
            low,
            jnp.concatenate([value, other], dim),
            jnp.concatenate([other, value], dim),
        )
        bit *= 2
    return value


def tree_scatter(buffer, axis, count, order):
    index = lax.axis_index(axis)
    width = buffer.shape[1]
    levels = len(order)
    cube = buffer.reshape((2,) * levels + (width,))
    natural = [count // (2 ** (k + 1)) for k in range(levels)]
    cube = cube.transpose([natural.index(bit) for bit in order] + [levels])
    buffer = cube.reshape(count, width)
    for bit in order:
        rows = buffer.shape[0]
        halves = buffer.reshape(2, rows // 2, width)
        own = (index // bit) % 2
        keep = lax.dynamic_index_in_dim(halves, own, axis=0, keepdims=False)
        send = lax.dynamic_index_in_dim(halves, 1 - own, axis=0, keepdims=False)
        received = lax.ppermute(send.astype(jnp.bfloat16), axis, xor_pairs(count, bit))
        buffer = keep.astype(jnp.float32) + received.astype(jnp.float32)
    return buffer


def halving_order(count):
    return [count // (2 ** (k + 1)) for k in range(count.bit_length() - 1)]


def local(
    stream,
    normed,
    query_weight,
    key_weight,
    value_weight,
    out_weight,
    norm_gain,
    proj_weight,
    images,
):
    seq_count = normed.shape[0]
    length = normed.shape[1]
    col_count = query_weight.shape[1]
    feat_share = stream.shape[2]
    head_size = D // H
    scale_head = head_size ** (-0.5)
    dp_parts = lax.psum(1, "dp")
    t_parts = lax.psum(1, "tensor")
    t_index = lax.axis_index("tensor")
    gain_full = tree_gather(norm_gain, "tensor", t_parts, 0).astype(jnp.float32)
    gathered = tree_gather(images, "dp", dp_parts, 0).astype(jnp.float32)
    image_unit = gathered / jnp.sqrt(jnp.sum(gathered * gathered, axis=-1, keepdims=True) + EPSILON)

    queries = split_heads(project(normed, query_weight), head_size)
    keys_all = split_heads(project(normed, key_weight), head_size)
    values_all = split_heads(project(normed, value_weight), head_size)
    scores = (
        jnp.einsum("bqhd,bkhd->bhqk", queries, keys_all, preferred_element_type=jnp.float32)
        * scale_head
    )
    row_max = jnp.max(scores, axis=-1, keepdims=True)
    exp_scores = jnp.exp(scores - row_max)
    attn_prob = exp_scores / jnp.sum(exp_scores, axis=-1, keepdims=True)
    attn_half = attn_prob.astype(jnp.bfloat16)
    heads_out = jnp.einsum(
        "bhqk,bkhd->bqhd", attn_half, values_all, preferred_element_type=jnp.float32
    )
    head_concat = heads_out.astype(jnp.bfloat16).reshape(seq_count, length, col_count)
    blocks = jnp.einsum(
        "blc,cjw->jblw",
        head_concat,
        out_weight.reshape(col_count, t_parts, feat_share),
        preferred_element_type=jnp.float32,
    ).astype(jnp.bfloat16)
    arrived = lax.all_to_all(blocks, "tensor", 0, 0, tiled=True)
    own_residual = stream.astype(jnp.float32) + jnp.sum(arrived.astype(jnp.float32), axis=0)
    residual = lax.all_gather(
        own_residual.astype(jnp.bfloat16), "tensor", axis=2, tiled=True
    ).astype(jnp.float32)
    center = jnp.mean(residual, axis=-1, keepdims=True)
    offset = residual - center
    variance = jnp.mean(offset * offset, axis=-1, keepdims=True)
    inv_std = lax.rsqrt(variance + EPSILON)
    normal_feat = offset * inv_std
    pooled_full = jnp.mean(normal_feat * gain_full, axis=1)
    pooled = lax.dynamic_slice_in_dim(pooled_full, t_index * feat_share, feat_share, 1).astype(
        jnp.bfloat16
    )
    embedded = tree_sum(
        jnp.dot(pooled, proj_weight, preferred_element_type=jnp.float32), "tensor", t_parts
    )
    embed_norm = jnp.sqrt(jnp.sum(embedded * embedded, axis=-1, keepdims=True) + EPSILON)
    spectra = embedded / embed_norm
    logits = SCALE_LOGIT * jnp.dot(spectra, image_unit.T, precision=HIGH)
    own_start = lax.axis_index("dp") * seq_count
    columns = jnp.arange(logits.shape[1], dtype=jnp.int32)
    own_rows = own_start + jnp.arange(seq_count, dtype=jnp.int32)
    matches = (columns[None, :] == own_rows[:, None]).astype(jnp.float32)
    exp_logits = jnp.exp(logits)
    row_lse = jnp.log(jnp.sum(exp_logits, axis=1))
    diagonal = jnp.sum(logits * matches, axis=1)
    local_loss = 0.5 * jnp.sum(row_lse) - jnp.sum(diagonal)
    loss_terms = tree_sum(
        jnp.concatenate([jnp.sum(exp_logits, axis=0), local_loss[None]]), "dp", dp_parts
    )
    col_total = loss_terms[:-1]
    loss_sum = loss_terms[-1]
    col_lse = jnp.log(col_total)
    mean_loss = (loss_sum + 0.5 * jnp.sum(col_lse)) / logits.shape[1]
    grad_logits = GRAD_SCALE * (
        0.5 * jnp.exp(logits - row_lse[:, None])
        + 0.5 * jnp.exp(logits - col_lse[None, :])
        - matches
    )
    grad_spec = SCALE_LOGIT * jnp.dot(grad_logits, image_unit, precision=HIGH)
    radial = jnp.sum(spectra * grad_spec, axis=-1, keepdims=True)
    grad_embed = ((grad_spec - spectra * radial) / embed_norm).astype(jnp.bfloat16)
    grad_proj = lax.dot_general(
        pooled, grad_embed, (((0,), (0,)), ((), ())), preferred_element_type=jnp.float32
    )
    grad_pooled = lax.dot_general(
        grad_embed, proj_weight, (((1,), (1,)), ((), ())), preferred_element_type=jnp.float32
    )
    grad_pooled_full = tree_gather(grad_pooled, "tensor", t_parts, 1)
    grad_normal = jnp.broadcast_to(
        grad_pooled_full[:, None, :] / length, normal_feat.shape
    ) * gain_full
    mean_one = jnp.mean(grad_normal, axis=-1, keepdims=True)
    mean_two = jnp.mean(grad_normal * normal_feat, axis=-1, keepdims=True)
    piece_rows = (inv_std * (grad_normal - mean_one - normal_feat * mean_two)).astype(jnp.bfloat16)
    grad_heads = jnp.einsum(
        "blw,cw->blc", piece_rows, out_weight, preferred_element_type=jnp.float32
    )
    grad_out = jnp.einsum("blc,blw->cw", head_concat, piece_rows, preferred_element_type=jnp.float32)
    grad_heads = split_heads(grad_heads.astype(jnp.bfloat16), head_size)
    grad_probs = jnp.einsum(
        "bqhd,bkhd->bhqk", grad_heads, values_all, preferred_element_type=jnp.float32
    )
    row_dot = jnp.sum(attn_prob * grad_probs, axis=-1, keepdims=True)
    grad_scores = (attn_prob * (grad_probs - row_dot) * scale_head).astype(jnp.bfloat16)
    grad_q = (
        jnp.einsum("bhqk,bkhd->bqhd", grad_scores, keys_all, preferred_element_type=jnp.float32)
        .astype(jnp.bfloat16)
        .reshape(seq_count, length, col_count)
    )
    grad_k = (
        jnp.einsum("bhqk,bqhd->bkhd", grad_scores, queries, preferred_element_type=jnp.float32)
        .astype(jnp.bfloat16)
        .reshape(seq_count, length, col_count)
    )
    grad_v = (
        jnp.einsum("bhqk,bqhd->bkhd", attn_half, grad_heads, preferred_element_type=jnp.float32)
        .astype(jnp.bfloat16)
        .reshape(seq_count, length, col_count)
    )
    back_input = jnp.einsum("blc,dc->bld", grad_q, query_weight, preferred_element_type=jnp.float32)
    back_input = back_input + jnp.einsum(
        "blc,dc->bld", grad_k, key_weight, preferred_element_type=jnp.float32
    )
    back_input = back_input + jnp.einsum(
        "blc,dc->bld", grad_v, value_weight, preferred_element_type=jnp.float32
    )
    late_pieces = [
        chunks_cols(grad_out.astype(jnp.bfloat16), dp_parts),
        chunks_cols(grad_proj.astype(jnp.bfloat16), dp_parts),
    ]
    late_reduced = tree_scatter(jnp.concatenate(late_pieces, axis=1), "dp", dp_parts, halving_order(dp_parts))
    grad_query = jnp.einsum("bld,blc->dc", normed, grad_q, preferred_element_type=jnp.float32)
    grad_key = jnp.einsum("bld,blc->dc", normed, grad_k, preferred_element_type=jnp.float32)
    grad_value = jnp.einsum("bld,blc->dc", normed, grad_v, preferred_element_type=jnp.float32)
    early_pieces = [
        chunks_rows(grad_query.astype(jnp.bfloat16), dp_parts),
        chunks_rows(grad_key.astype(jnp.bfloat16), dp_parts),
        chunks_rows(grad_value.astype(jnp.bfloat16), dp_parts),
    ]
    back_half, early_joined = lax.optimization_barrier(
        (back_input.astype(jnp.bfloat16), jnp.concatenate(early_pieces, axis=1))
    )
    grad_normed = lax.psum_scatter(back_half, "tensor", scatter_dimension=2, tiled=True)
    early_reduced = tree_scatter(early_joined, "dp", dp_parts, halving_order(dp_parts))
    widths = [piece.shape[1] for piece in early_pieces + late_pieces]
    reduced = jnp.concatenate([early_reduced, late_reduced], axis=1)
    outs = []
    start = 0
    for width in widths:
        outs.append(reduced[0, start:start + width])
        start += width
    rows_q = D // dp_parts
    grad_query_out = outs[0].reshape(rows_q, col_count)
    grad_key_out = outs[1].reshape(rows_q, col_count)
    grad_value_out = outs[2].reshape(rows_q, col_count)
    grad_out_out = outs[3].reshape(grad_out.shape[0], grad_out.shape[1] // dp_parts)
    grad_proj_out = outs[4].reshape(grad_proj.shape[0], grad_proj.shape[1] // dp_parts)
    return (
        mean_loss,
        grad_normed,
        grad_query_out,
        grad_key_out,
        grad_value_out,
        grad_out_out,
        grad_proj_out,
    )


def solution(mesh):
    return jax.shard_map(
        local,
        mesh=mesh,
        in_specs=(
            P("dp", None, "tensor"),
            P("dp", None, None),
            P(None, "tensor"),
            P(None, "tensor"),
            P(None, "tensor"),
            P("tensor", None),
            P("tensor"),
            P("tensor", None),
            P("dp", None),
        ),
        out_specs=(
            P(),
            P("dp", None, "tensor"),
            P("dp", "tensor"),
            P("dp", "tensor"),
            P("dp", "tensor"),
            P("tensor", "dp"),
            P("tensor", "dp"),
        ),
        check_vma=False,
    )
```

```python
import jax
import jax.numpy as jnp
from jax import lax
from jax.sharding import PartitionSpec as P

D = 2048
H = 16


SCALE_LOGIT = 14.0
GRAD_SCALE = 256.0
EPSILON = 1e-05
HIGH = lax.Precision.HIGHEST


def project(inputs, weight):
    return jnp.einsum("bld,dc->blc", inputs, weight, preferred_element_type=jnp.float32).astype(
        jnp.bfloat16
    )


def split_heads(values, head_size):
    return values.reshape(values.shape[0], values.shape[1], values.shape[2] // head_size, head_size)


def chunks_rows(grad, parts):
    rows, cols = grad.shape
    return grad.reshape(parts, (rows // parts) * cols)


def chunks_cols(grad, parts):
    rows, cols = grad.shape
    return grad.reshape(rows, parts, cols // parts).transpose(1, 0, 2).reshape(parts, -1)


def xor_pairs(count, bit):
    return [(i, i ^ bit) for i in range(count)]


def tree_sum(value, axis, count):
    bit = 1
    while bit < count:
        value = value + lax.ppermute(value, axis, xor_pairs(count, bit))
        bit *= 2
    return value


def tree_gather(value, axis, count, dim):
    index = lax.axis_index(axis)
    bit = 1
    while bit < count:
        other = lax.ppermute(value, axis, xor_pairs(count, bit))
        low = (index // bit) % 2 == 0
        value = jnp.where(
            low,
            jnp.concatenate([value, other], dim),
            jnp.concatenate([other, value], dim),
        )
        bit *= 2
    return value


def tree_scatter(buffer, axis, count, order):
    index = lax.axis_index(axis)
    width = buffer.shape[1]
    levels = len(order)
    cube = buffer.reshape((2,) * levels + (width,))
    natural = [count // (2 ** (k + 1)) for k in range(levels)]
    cube = cube.transpose([natural.index(bit) for bit in order] + [levels])
    buffer = cube.reshape(count, width)
    for bit in order:
        rows = buffer.shape[0]
        halves = buffer.reshape(2, rows // 2, width)
        own = (index // bit) % 2
        keep = lax.dynamic_index_in_dim(halves, own, axis=0, keepdims=False)
        send = lax.dynamic_index_in_dim(halves, 1 - own, axis=0, keepdims=False)
        received = lax.ppermute(send.astype(jnp.bfloat16), axis, xor_pairs(count, bit))
        buffer = keep.astype(jnp.float32) + received.astype(jnp.float32)
    return buffer


def halving_order(count):
    return [count // (2 ** (k + 1)) for k in range(count.bit_length() - 1)]


def local(
    stream,
    normed,
    query_weight,
    key_weight,
    value_weight,
    out_weight,
    norm_gain,
    proj_weight,
    images,
):
    seq_count = normed.shape[0]
    length = normed.shape[1]
    col_count = query_weight.shape[1]
    feat_share = stream.shape[2]
    head_size = D // H
    scale_head = head_size ** (-0.5)
    dp_parts = lax.psum(1, "dp")
    t_parts = lax.psum(1, "tensor")
    t_index = lax.axis_index("tensor")
    gain_full = tree_gather(norm_gain, "tensor", t_parts, 0).astype(jnp.float32)
    gathered = tree_gather(images, "dp", dp_parts, 0).astype(jnp.float32)
    image_unit = gathered / jnp.sqrt(jnp.sum(gathered * gathered, axis=-1, keepdims=True) + EPSILON)

    queries = split_heads(project(normed, query_weight), head_size)
    keys_all = split_heads(project(normed, key_weight), head_size)
    values_all = split_heads(project(normed, value_weight), head_size)
    scores = (
        jnp.einsum("bqhd,bkhd->bhqk", queries, keys_all, preferred_element_type=jnp.float32)
        * scale_head
    )
    row_max = jnp.max(scores, axis=-1, keepdims=True)
    exp_scores = jnp.exp(scores - row_max)
    attn_prob = exp_scores / jnp.sum(exp_scores, axis=-1, keepdims=True)
    attn_half = attn_prob.astype(jnp.bfloat16)
    heads_out = jnp.einsum(
        "bhqk,bkhd->bqhd", attn_half, values_all, preferred_element_type=jnp.float32
    )
    head_concat = heads_out.astype(jnp.bfloat16).reshape(seq_count, length, col_count)
    blocks = jnp.einsum(
        "blc,cjw->jblw",
        head_concat,
        out_weight.reshape(col_count, t_parts, feat_share),
        preferred_element_type=jnp.float32,
    ).astype(jnp.bfloat16)
    arrived = lax.all_to_all(blocks, "tensor", 0, 0, tiled=True)
    own_residual = stream.astype(jnp.float32) + jnp.sum(arrived.astype(jnp.float32), axis=0)
    residual = lax.all_gather(
        own_residual.astype(jnp.bfloat16), "tensor", axis=2, tiled=True
    ).astype(jnp.float32)
    center = jnp.mean(residual, axis=-1, keepdims=True)
    offset = residual - center
    variance = jnp.mean(offset * offset, axis=-1, keepdims=True)
    inv_std = lax.rsqrt(variance + EPSILON)
    normal_feat = offset * inv_std
    pooled_full = jnp.mean(normal_feat * gain_full, axis=1)
    pooled = lax.dynamic_slice_in_dim(pooled_full, t_index * feat_share, feat_share, 1).astype(
        jnp.bfloat16
    )
    embedded = tree_sum(
        jnp.dot(pooled, proj_weight, preferred_element_type=jnp.float32), "tensor", t_parts
    )
    embed_norm = jnp.sqrt(jnp.sum(embedded * embedded, axis=-1, keepdims=True) + EPSILON)
    spectra = embedded / embed_norm
    logits = SCALE_LOGIT * jnp.dot(spectra, image_unit.T, precision=HIGH)
    own_start = lax.axis_index("dp") * seq_count
    columns = jnp.arange(logits.shape[1], dtype=jnp.int32)
    own_rows = own_start + jnp.arange(seq_count, dtype=jnp.int32)
    matches = (columns[None, :] == own_rows[:, None]).astype(jnp.float32)
    exp_logits = jnp.exp(logits)
    row_lse = jnp.log(jnp.sum(exp_logits, axis=1))
    diagonal = jnp.sum(logits * matches, axis=1)
    local_loss = 0.5 * jnp.sum(row_lse) - jnp.sum(diagonal)
    loss_terms = tree_sum(
        jnp.concatenate([jnp.sum(exp_logits, axis=0), local_loss[None]]), "dp", dp_parts
    )
    col_total = loss_terms[:-1]
    loss_sum = loss_terms[-1]
    col_lse = jnp.log(col_total)
    mean_loss = (loss_sum + 0.5 * jnp.sum(col_lse)) / logits.shape[1]
    grad_logits = GRAD_SCALE * (
        0.5 * jnp.exp(logits - row_lse[:, None])
        + 0.5 * jnp.exp(logits - col_lse[None, :])
        - matches
    )
    grad_spec = SCALE_LOGIT * jnp.dot(grad_logits, image_unit, precision=HIGH)
    radial = jnp.sum(spectra * grad_spec, axis=-1, keepdims=True)
    grad_embed = ((grad_spec - spectra * radial) / embed_norm).astype(jnp.bfloat16)
    grad_proj = lax.dot_general(
        pooled, grad_embed, (((0,), (0,)), ((), ())), preferred_element_type=jnp.float32
    )
    grad_pooled = lax.dot_general(
        grad_embed, proj_weight, (((1,), (1,)), ((), ())), preferred_element_type=jnp.float32
    )
    grad_pooled_full = tree_gather(grad_pooled, "tensor", t_parts, 1)
    grad_normal = jnp.broadcast_to(
        grad_pooled_full[:, None, :] / length, normal_feat.shape
    ) * gain_full
    mean_one = jnp.mean(grad_normal, axis=-1, keepdims=True)
    mean_two = jnp.mean(grad_normal * normal_feat, axis=-1, keepdims=True)
    piece_rows = (inv_std * (grad_normal - mean_one - normal_feat * mean_two)).astype(jnp.bfloat16)
    grad_heads = jnp.einsum(
        "blw,cw->blc", piece_rows, out_weight, preferred_element_type=jnp.float32
    )
    grad_out = jnp.einsum("blc,blw->cw", head_concat, piece_rows, preferred_element_type=jnp.float32)
    grad_heads = split_heads(grad_heads.astype(jnp.bfloat16), head_size)
    grad_probs = jnp.einsum(
        "bqhd,bkhd->bhqk", grad_heads, values_all, preferred_element_type=jnp.float32
    )
    row_dot = jnp.sum(attn_prob * grad_probs, axis=-1, keepdims=True)
    grad_scores = (attn_prob * (grad_probs - row_dot) * scale_head).astype(jnp.bfloat16)
    grad_q = (
        jnp.einsum("bhqk,bkhd->bqhd", grad_scores, keys_all, preferred_element_type=jnp.float32)
        .astype(jnp.bfloat16)
        .reshape(seq_count, length, col_count)
    )
    grad_k = (
        jnp.einsum("bhqk,bqhd->bkhd", grad_scores, queries, preferred_element_type=jnp.float32)
        .astype(jnp.bfloat16)
        .reshape(seq_count, length, col_count)
    )
    grad_v = (
        jnp.einsum("bhqk,bqhd->bkhd", attn_half, grad_heads, preferred_element_type=jnp.float32)
        .astype(jnp.bfloat16)
        .reshape(seq_count, length, col_count)
    )
    back_input = jnp.einsum("blc,dc->bld", grad_q, query_weight, preferred_element_type=jnp.float32)
    back_input = back_input + jnp.einsum(
        "blc,dc->bld", grad_k, key_weight, preferred_element_type=jnp.float32
    )
    back_input = back_input + jnp.einsum(
        "blc,dc->bld", grad_v, value_weight, preferred_element_type=jnp.float32
    )
    late_pieces = [
        chunks_cols(grad_out.astype(jnp.bfloat16), dp_parts),
        chunks_cols(grad_proj.astype(jnp.bfloat16), dp_parts),
    ]
    late_reduced = tree_scatter(jnp.concatenate(late_pieces, axis=1), "dp", dp_parts, halving_order(dp_parts))
    grad_value = jnp.einsum("bld,blc->dc", normed, grad_v, preferred_element_type=jnp.float32)
    value_piece = chunks_rows(grad_value.astype(jnp.bfloat16), dp_parts)
    value_reduced = tree_scatter(value_piece, "dp", dp_parts, halving_order(dp_parts))
    grad_query = jnp.einsum("bld,blc->dc", normed, grad_q, preferred_element_type=jnp.float32)
    grad_key = jnp.einsum("bld,blc->dc", normed, grad_k, preferred_element_type=jnp.float32)
    early_pieces = [
        chunks_rows(grad_query.astype(jnp.bfloat16), dp_parts),
        chunks_rows(grad_key.astype(jnp.bfloat16), dp_parts),
    ]
    back_half, early_joined = lax.optimization_barrier(
        (back_input.astype(jnp.bfloat16), jnp.concatenate(early_pieces, axis=1))
    )
    grad_normed = lax.psum_scatter(back_half, "tensor", scatter_dimension=2, tiled=True)
    early_reduced = tree_scatter(early_joined, "dp", dp_parts, halving_order(dp_parts))
    early_pieces = early_pieces + [value_piece]
    early_reduced = jnp.concatenate([early_reduced, value_reduced], axis=1)
    widths = [piece.shape[1] for piece in early_pieces + late_pieces]
    reduced = jnp.concatenate([early_reduced, late_reduced], axis=1)
    outs = []
    start = 0
    for width in widths:
        outs.append(reduced[0, start:start + width])
        start += width
    rows_q = D // dp_parts
    grad_query_out = outs[0].reshape(rows_q, col_count)
    grad_key_out = outs[1].reshape(rows_q, col_count)
    grad_value_out = outs[2].reshape(rows_q, col_count)
    grad_out_out = outs[3].reshape(grad_out.shape[0], grad_out.shape[1] // dp_parts)
    grad_proj_out = outs[4].reshape(grad_proj.shape[0], grad_proj.shape[1] // dp_parts)
    return (
        mean_loss,
        grad_normed,
        grad_query_out,
        grad_key_out,
        grad_value_out,
        grad_out_out,
        grad_proj_out,
    )


def solution(mesh):
    return jax.shard_map(
        local,
        mesh=mesh,
        in_specs=(
            P("dp", None, "tensor"),
            P("dp", None, None),
            P(None, "tensor"),
            P(None, "tensor"),
            P(None, "tensor"),
            P("tensor", None),
            P("tensor"),
            P("tensor", None),
            P("dp", None),
        ),
        out_specs=(
            P(),
            P("dp", None, "tensor"),
            P("dp", "tensor"),
            P("dp", "tensor"),
            P("dp", "tensor"),
            P("tensor", "dp"),
            P("tensor", "dp"),
        ),
        check_vma=False,
    )
```

```python
import jax
import jax.numpy as jnp
from jax import lax
from jax.sharding import PartitionSpec as P

D = 2048
H = 16


SCALE_LOGIT = 14.0
GRAD_SCALE = 256.0
EPSILON = 1e-05
HIGH = lax.Precision.HIGHEST


def project(inputs, weight):
    return jnp.einsum("bld,dc->blc", inputs, weight, preferred_element_type=jnp.float32).astype(
        jnp.bfloat16
    )


def split_heads(values, head_size):
    return values.reshape(values.shape[0], values.shape[1], values.shape[2] // head_size, head_size)


def chunks_rows(grad, parts):
    rows, cols = grad.shape
    return grad.reshape(parts, (rows // parts) * cols)


def chunks_cols(grad, parts):
    rows, cols = grad.shape
    return grad.reshape(rows, parts, cols // parts).transpose(1, 0, 2).reshape(parts, -1)


def xor_pairs(count, bit):
    return [(i, i ^ bit) for i in range(count)]


def tree_sum(value, axis, count):
    bit = 1
    while bit < count:
        value = value + lax.ppermute(value, axis, xor_pairs(count, bit))
        bit *= 2
    return value


def tree_gather(value, axis, count, dim):
    index = lax.axis_index(axis)
    bit = 1
    while bit < count:
        other = lax.ppermute(value, axis, xor_pairs(count, bit))
        low = (index // bit) % 2 == 0
        value = jnp.where(
            low,
            jnp.concatenate([value, other], dim),
            jnp.concatenate([other, value], dim),
        )
        bit *= 2
    return value


def tree_scatter(buffer, axis, count, order):
    index = lax.axis_index(axis)
    width = buffer.shape[1]
    levels = len(order)
    cube = buffer.reshape((2,) * levels + (width,))
    natural = [count // (2 ** (k + 1)) for k in range(levels)]
    cube = cube.transpose([natural.index(bit) for bit in order] + [levels])
    buffer = cube.reshape(count, width)
    for bit in order:
        rows = buffer.shape[0]
        halves = buffer.reshape(2, rows // 2, width)
        own = (index // bit) % 2
        keep = lax.dynamic_index_in_dim(halves, own, axis=0, keepdims=False)
        send = lax.dynamic_index_in_dim(halves, 1 - own, axis=0, keepdims=False)
        received = lax.ppermute(send.astype(jnp.bfloat16), axis, xor_pairs(count, bit))
        buffer = keep.astype(jnp.float32) + received.astype(jnp.float32)
    return buffer


def halving_order(count):
    return [count // (2 ** (k + 1)) for k in range(count.bit_length() - 1)]


def local(
    stream,
    normed,
    query_weight,
    key_weight,
    value_weight,
    out_weight,
    norm_gain,
    proj_weight,
    images,
):
    seq_count = normed.shape[0]
    length = normed.shape[1]
    col_count = query_weight.shape[1]
    feat_share = stream.shape[2]
    head_size = D // H
    scale_head = head_size ** (-0.5)
    dp_parts = lax.psum(1, "dp")
    t_parts = lax.psum(1, "tensor")
    t_index = lax.axis_index("tensor")
    gain_full = tree_gather(norm_gain, "tensor", t_parts, 0).astype(jnp.float32)
    gathered = tree_gather(images, "dp", dp_parts, 0).astype(jnp.float32)
    image_unit = gathered / jnp.sqrt(jnp.sum(gathered * gathered, axis=-1, keepdims=True) + EPSILON)

    queries = split_heads(project(normed, query_weight), head_size)
    keys_all = split_heads(project(normed, key_weight), head_size)
    values_all = split_heads(project(normed, value_weight), head_size)
    scores = (
        jnp.einsum("bqhd,bkhd->bhqk", queries, keys_all, preferred_element_type=jnp.float32)
        * scale_head
    )
    row_max = jnp.max(scores, axis=-1, keepdims=True)
    exp_scores = jnp.exp(scores - row_max)
    attn_prob = exp_scores / jnp.sum(exp_scores, axis=-1, keepdims=True)
    attn_half = attn_prob.astype(jnp.bfloat16)
    heads_out = jnp.einsum(
        "bhqk,bkhd->bqhd", attn_half, values_all, preferred_element_type=jnp.float32
    )
    head_concat = heads_out.astype(jnp.bfloat16).reshape(seq_count, length, col_count)
    blocks = jnp.einsum(
        "blc,cjw->jblw",
        head_concat,
        out_weight.reshape(col_count, t_parts, feat_share),
        preferred_element_type=jnp.float32,
    ).astype(jnp.bfloat16)
    arrived = lax.all_to_all(blocks, "tensor", 0, 0, tiled=True)
    own_residual = stream.astype(jnp.float32) + jnp.sum(arrived.astype(jnp.float32), axis=0)
    residual = lax.all_gather(
        own_residual.astype(jnp.bfloat16), "tensor", axis=2, tiled=True
    ).astype(jnp.float32)
    center = jnp.mean(residual, axis=-1, keepdims=True)
    offset = residual - center
    variance = jnp.mean(offset * offset, axis=-1, keepdims=True)
    inv_std = lax.rsqrt(variance + EPSILON)
    normal_feat = offset * inv_std
    pooled_full = jnp.mean(normal_feat * gain_full, axis=1)
    pooled = lax.dynamic_slice_in_dim(pooled_full, t_index * feat_share, feat_share, 1).astype(
        jnp.bfloat16
    )
    embedded = tree_sum(
        jnp.dot(pooled, proj_weight, preferred_element_type=jnp.float32), "tensor", t_parts
    )
    embed_norm = jnp.sqrt(jnp.sum(embedded * embedded, axis=-1, keepdims=True) + EPSILON)
    spectra = embedded / embed_norm
    logits = SCALE_LOGIT * jnp.dot(spectra, image_unit.T, precision=HIGH)
    own_start = lax.axis_index("dp") * seq_count
    columns = jnp.arange(logits.shape[1], dtype=jnp.int32)
    own_rows = own_start + jnp.arange(seq_count, dtype=jnp.int32)
    matches = (columns[None, :] == own_rows[:, None]).astype(jnp.float32)
    exp_logits = jnp.exp(logits)
    row_lse = jnp.log(jnp.sum(exp_logits, axis=1))
    diagonal = jnp.sum(logits * matches, axis=1)
    local_loss = 0.5 * jnp.sum(row_lse) - jnp.sum(diagonal)
    loss_terms = tree_sum(
        jnp.concatenate([jnp.sum(exp_logits, axis=0), local_loss[None]]), "dp", dp_parts
    )
    col_total = loss_terms[:-1]
    loss_sum = loss_terms[-1]
    col_lse = jnp.log(col_total)
    mean_loss = (loss_sum + 0.5 * jnp.sum(col_lse)) / logits.shape[1]
    grad_logits = GRAD_SCALE * (
        0.5 * jnp.exp(logits - row_lse[:, None])
        + 0.5 * jnp.exp(logits - col_lse[None, :])
        - matches
    )
    grad_spec = SCALE_LOGIT * jnp.dot(grad_logits, image_unit, precision=HIGH)
    radial = jnp.sum(spectra * grad_spec, axis=-1, keepdims=True)
    grad_embed = ((grad_spec - spectra * radial) / embed_norm).astype(jnp.bfloat16)
    grad_proj_t = lax.dot_general(
        grad_embed, pooled, (((0,), (0,)), ((), ())), preferred_element_type=jnp.float32
    )
    grad_pooled = lax.dot_general(
        grad_embed, proj_weight, (((1,), (1,)), ((), ())), preferred_element_type=jnp.float32
    )
    grad_pooled_full = tree_gather(grad_pooled, "tensor", t_parts, 1)
    grad_normal = jnp.broadcast_to(
        grad_pooled_full[:, None, :] / length, normal_feat.shape
    ) * gain_full
    mean_one = jnp.mean(grad_normal, axis=-1, keepdims=True)
    mean_two = jnp.mean(grad_normal * normal_feat, axis=-1, keepdims=True)
    piece_rows = (inv_std * (grad_normal - mean_one - normal_feat * mean_two)).astype(jnp.bfloat16)
    grad_heads = jnp.einsum(
        "blw,cw->blc", piece_rows, out_weight, preferred_element_type=jnp.float32
    )
    grad_out_t = jnp.einsum("blw,blc->wc", piece_rows, head_concat, preferred_element_type=jnp.float32)
    grad_heads = split_heads(grad_heads.astype(jnp.bfloat16), head_size)
    grad_probs = jnp.einsum(
        "bqhd,bkhd->bhqk", grad_heads, values_all, preferred_element_type=jnp.float32
    )
    row_dot = jnp.sum(attn_prob * grad_probs, axis=-1, keepdims=True)
    grad_scores = (attn_prob * (grad_probs - row_dot) * scale_head).astype(jnp.bfloat16)
    grad_q = (
        jnp.einsum("bhqk,bkhd->bqhd", grad_scores, keys_all, preferred_element_type=jnp.float32)
        .astype(jnp.bfloat16)
        .reshape(seq_count, length, col_count)
    )
    grad_k = (
        jnp.einsum("bhqk,bqhd->bkhd", grad_scores, queries, preferred_element_type=jnp.float32)
        .astype(jnp.bfloat16)
        .reshape(seq_count, length, col_count)
    )
    grad_v = (
        jnp.einsum("bhqk,bqhd->bkhd", attn_half, grad_heads, preferred_element_type=jnp.float32)
        .astype(jnp.bfloat16)
        .reshape(seq_count, length, col_count)
    )
    back_input = jnp.einsum("blc,dc->bld", grad_q, query_weight, preferred_element_type=jnp.float32)
    back_input = back_input + jnp.einsum(
        "blc,dc->bld", grad_k, key_weight, preferred_element_type=jnp.float32
    )
    back_input = back_input + jnp.einsum(
        "blc,dc->bld", grad_v, value_weight, preferred_element_type=jnp.float32
    )
    late_pieces = [
        chunks_rows(grad_out_t.astype(jnp.bfloat16), dp_parts),
        chunks_rows(grad_proj_t.astype(jnp.bfloat16), dp_parts),
    ]
    late_reduced = tree_scatter(jnp.concatenate(late_pieces, axis=1), "dp", dp_parts, halving_order(dp_parts))
    grad_query = jnp.einsum("bld,blc->dc", normed, grad_q, preferred_element_type=jnp.float32)
    grad_key = jnp.einsum("bld,blc->dc", normed, grad_k, preferred_element_type=jnp.float32)
    grad_value = jnp.einsum("bld,blc->dc", normed, grad_v, preferred_element_type=jnp.float32)
    early_pieces = [
        chunks_rows(grad_query.astype(jnp.bfloat16), dp_parts),
        chunks_rows(grad_key.astype(jnp.bfloat16), dp_parts),
        chunks_rows(grad_value.astype(jnp.bfloat16), dp_parts),
    ]
    back_half, early_joined = lax.optimization_barrier(
        (back_input.astype(jnp.bfloat16), jnp.concatenate(early_pieces, axis=1))
    )
    grad_normed = lax.psum_scatter(back_half, "tensor", scatter_dimension=2, tiled=True)
    early_reduced = tree_scatter(early_joined, "dp", dp_parts, halving_order(dp_parts))
    widths = [piece.shape[1] for piece in early_pieces + late_pieces]
    reduced = jnp.concatenate([early_reduced, late_reduced], axis=1)
    outs = []
    start = 0
    for width in widths:
        outs.append(reduced[0, start:start + width])
        start += width
    rows_q = D // dp_parts
    grad_query_out = outs[0].reshape(rows_q, col_count)
    grad_key_out = outs[1].reshape(rows_q, col_count)
    grad_value_out = outs[2].reshape(rows_q, col_count)
    grad_out_out = outs[3].reshape(grad_out_t.shape[0] // dp_parts, grad_out_t.shape[1]).T
    grad_proj_out = outs[4].reshape(grad_proj_t.shape[0] // dp_parts, grad_proj_t.shape[1]).T
    return (
        mean_loss,
        grad_normed,
        grad_query_out,
        grad_key_out,
        grad_value_out,
        grad_out_out,
        grad_proj_out,
    )


def solution(mesh):
    return jax.shard_map(
        local,
        mesh=mesh,
        in_specs=(
            P("dp", None, "tensor"),
            P("dp", None, None),
            P(None, "tensor"),
            P(None, "tensor"),
            P(None, "tensor"),
            P("tensor", None),
            P("tensor"),
            P("tensor", None),
            P("dp", None),
        ),
        out_specs=(
            P(),
            P("dp", None, "tensor"),
            P("dp", "tensor"),
            P("dp", "tensor"),
            P("dp", "tensor"),
            P("tensor", "dp"),
            P("tensor", "dp"),
        ),
        check_vma=False,
    )
```
